32 devices in a mesh: dp: 8 (over z, x), vocab: 4 (over y, core).
Axes of the slice: x: 2, y: 2, z: 4, core: 2. Of those that a mesh axis runs over, the one named last changes fastest.
Arguments:
- hidden: bfloat16 [256, 16384], P('dp', 'vocab'), may hold values from -10 to 10
- head_weight: bfloat16 [16384, 16384], P('vocab', 'dp'), may hold values from -0.1171875 to 0.1171875
- lengths: int32 [8], replicated, may hold values from 1 to 32, 160 in all
- targets: int32 [256], replicated, may hold values from 0 to 16383
- policy_logprobs: float32 [256], P('dp'), may hold values from -18 to -6
Outputs:
- ref_logprob: float32 [256], P('dp')
- token_kl: float32 [256], P('dp')
The draws below stay inside these ranges and needn't reach their ends.
Inputs may be any that keep to these rules, and one draw needn't show every extreme that they name: The 8 lengths sum to exactly 160, and the longest is exactly 32.
All inputs are finite; a program needn't handle non-finite values.
Results may differ from the reference program's by a relative error of at most 0.0003.
Values may be sent and summed in bfloat16 or wider, within the bound.
No kernel may reach another device: no remote copies, remote signals or barrier semaphores. Data moves between devices by JAX's collectives and lax.ppermute only.
A program may use at most 64 MiB of HBM per device.

```python
import math
import jax
import jax.numpy as jnp
import numpy as np

D = 16384
MB = 8
V = 16384
TOTAL = 256
SLOTS = 32
LIVE = 160


def draw_hidden(key, part):
    key_noise, key_scale = jax.random.split(jax.random.fold_in(key, 23), 2)
    noise_field = jnp.clip(jax.random.normal(key_noise, (TOTAL, D), jnp.float32), -4.0, 4.0)
    row_scale = jnp.exp(jax.random.uniform(key_scale, (TOTAL, 1), jnp.float32, math.log(0.5), math.log(2.5)))
    values = noise_field * row_scale
    return values.astype(jnp.bfloat16)


def draw_head_weight(key, part):
    key_noise, key_scale = jax.random.split(jax.random.fold_in(key, 11), 2)
    noise_field = jnp.clip(jax.random.normal(key_noise, (D, V), jnp.float32), -4.0, 4.0)
    column_ids = jnp.arange(V)
    column_scale = jnp.exp(jax.random.uniform(key_scale, (V,), jnp.float32, math.log(0.6), math.log(1.8)))
    column_scale = column_scale * (1.0 + 0.3 * column_ids.astype(jnp.float32) / V)
    values = noise_field * column_scale[None, :] * (1.5 / math.sqrt(D))
    return values.astype(jnp.bfloat16)


def place_ends(result, rng, least, top_value):
    index_at = [jax.random.randint(jax.random.fold_in(rng, axis), (), 0, length) for axis, length in enumerate(result.shape)]
    main_axis = result.shape.index(max(result.shape))
    beside = index_at[:main_axis] + [(index_at[main_axis] + 1) % result.shape[main_axis]] + index_at[main_axis + 1:]
    return result.at[tuple(index_at)].set(least).at[tuple(beside)].set(top_value)


def shard_levels(rng, shape, cuts, low, largest):
    loudness, own = 1.0, jax.random.fold_in(rng, 6)
    for position, parts in cuts:
        heights = jnp.exp(jax.random.uniform(jax.random.fold_in(own, position), (parts,), jnp.float32, low / len(cuts), largest / len(cuts)))
        loudness = loudness * jnp.repeat(heights, shape[position] // parts).reshape([-1 if axis == position else 1 for axis in range(len(shape))])
    return loudness


def split_up(amount, total, bound, skew):
    weights = [(1 << 20) // math.isqrt(grade ** skew) + 1 for grade in range(2, amount + 1)]
    surplus, holding = total - bound - (amount - 1), [1] * (amount - 1)
    while surplus > 0:
        candidates = [i for i in range(amount - 1) if holding[i] < bound]
        mass, budget = sum([weights[i] for i in candidates]), surplus
        for i in candidates:
            addition = min(bound - holding[i], max(1, budget * weights[i] // mass), surplus)
            holding[i] = holding[i] + addition
            surplus = surplus - addition
    return np.array([bound] + holding)


def ragged_sizes(key, count, total, most, lean):
    if count == 2:
        one = jax.random.randint(key, (), max(1, total - most), min(most, total - 1) + 1)
        return jnp.stack([one, total - one])
    tallies = jnp.asarray(split_up(count, total, most, lean), jnp.int32)
    couples = (count - 1) // 2
    giver, receiver = tallies[1:1 + 2 * couples:2], tallies[2:2 + 2 * couples:2]
    margin = jnp.minimum(giver - 1, most - receiver)
    passed = jax.random.randint(jax.random.fold_in(key, 1), (couples,), 0, 1 << 20) % (margin + 1)
    tallies = tallies.at[1:1 + 2 * couples:2].set(giver - passed).at[2:2 + 2 * couples:2].set(receiver + passed)
    return tallies[jax.random.permutation(jax.random.fold_in(key, 2), count)]


def setup_inputs(seed: int = 0) -> dict:
    key_list = jax.random.split(jax.random.key(seed), 6)
    hidden = draw_hidden(jax.random.fold_in(key_list[5], 71), 0)
    head_weight = draw_head_weight(jax.random.fold_in(key_list[5], 71), 0)
    lengths = ragged_sizes(key_list[2], MB, LIVE, SLOTS, 2).astype(jnp.int32)
    targets = place_ends(jax.random.randint(key_list[3], (TOTAL,), 0, V), jax.random.fold_in(key_list[3], 1), 0, V - 1).astype(jnp.int32)
    policy_logprobs = jnp.clip(-18.0 + 12.0 * jax.random.uniform(key_list[4], (TOTAL,), jnp.float32) ** shard_levels(key_list[4], (TOTAL,), ((0, 8),), -0.2, 0.2), -18.0, -6.0)
    return dict(hidden=hidden, head_weight=head_weight, lengths=lengths, targets=targets, policy_logprobs=policy_logprobs)


def reference(hidden, head_weight, lengths, targets, policy_logprobs):
    logits = jnp.dot(hidden, head_weight, preferred_element_type=jnp.float32)
    highest = jnp.max(logits, axis=1)
    log_total = highest + jnp.log(jnp.sum(jnp.exp(logits - highest[:, None]), axis=1))
    picked = jnp.take_along_axis(logits, targets.astype(jnp.int32)[:, None], axis=1)[:, 0]
    row_ids = jnp.arange(TOTAL, dtype=jnp.int32)
    batch_of = row_ids // SLOTS
    slot_of = row_ids % SLOTS
    is_live = slot_of < jnp.take(lengths, batch_of)
    ref_logprob = jnp.where(is_live, picked - log_total, jnp.float32(0.0))
    ratio_log = jnp.clip(ref_logprob - policy_logprobs, -20.0, 20.0)
    kl_value = jnp.where(is_live, jnp.minimum(jnp.exp(ratio_log) - ratio_log - 1.0, 10.0), jnp.float32(0.0))
    return ref_logprob, kl_value
```

```python
import numpy as np
import jax
import jax.numpy as jnp
from jax import lax
from jax.sharding import PartitionSpec as P

MB = 8


def dp_ring(mesh):
    size = mesh.shape["dp"]
    try:
        coords = [tuple(dev.coords) for dev in mesh.devices[:, 0]]
        xs = sorted({c[0] for c in coords})
        zs = sorted({c[2] for c in coords})
        if len(xs) * len(zs) != size or len(zs) % 2:
            raise ValueError
        where = {(c[0], c[2]): i for i, c in enumerate(coords)}
        order = [where[(xs[0], z)] for z in zs]
        for row, z in enumerate(reversed(zs)):
            cols = xs[1:] if row % 2 == 0 else list(reversed(xs[1:]))
            order += [where[(x, z)] for x in cols]
        if sorted(order) != list(range(size)):
            raise ValueError
        return order
    except Exception:
        return list(range(size))


def ring_gather(block, ring):
    size = len(ring)
    pos_of = np.argsort(np.asarray(ring))
    fwd = [(ring[i], ring[(i + 1) % size]) for i in range(size)]
    bwd = [(ring[(i + 1) % size], ring[i]) for i in range(size)]
    slots = [None] * size
    slots[0] = block
    ahead, behind = block, block
    for step in range(1, size // 2 + 1):
        ahead = lax.ppermute(ahead, "dp", fwd)
        slots[step] = ahead
        if step < size - step:
            behind = lax.ppermute(behind, "dp", bwd)
            slots[size - step] = behind
    stacked = jnp.stack(slots)
    me = jnp.asarray(pos_of, jnp.int32)[lax.axis_index("dp")]
    pick = (me - jnp.asarray(pos_of, jnp.int32)) % size
    return jnp.take(stacked, pick, axis=0).reshape(-1, block.shape[1])


def halving_scatter(partial, size):
    me = lax.axis_index("vocab")
    first = jnp.int32(0)
    bit = 1
    while bit < size:
        half = partial.shape[0] // 2
        pairs = partial.reshape(2, half, partial.shape[1])
        side = (me // bit) % 2
        keep = jnp.take(pairs, side, axis=0)
        send = jnp.take(pairs, 1 - side, axis=0)
        got = lax.ppermute(send, "vocab", [(i, i ^ bit) for i in range(size)])
        partial = keep + got
        first = first + side * half
        bit *= 2
    return partial, first


def merge_stats(stats, size):
    bit = 1
    while bit < size:
        other = lax.ppermute(stats, "dp", [(i, i ^ bit) for i in range(size)])
        top = jnp.maximum(stats[0], other[0])
        total = stats[1] * jnp.exp(stats[0] - top) + other[1] * jnp.exp(other[0] - top)
        stats = jnp.stack([top, total, stats[2] + other[2]])
        bit *= 2
    return stats


def doubling_gather(values, first, size):
    me = lax.axis_index("vocab")
    total = values.shape[0] * size
    out = jnp.zeros((total,), values.dtype)
    out = lax.dynamic_update_slice(out, values, (first,))
    bit = 1
    while bit < size:
        other = lax.ppermute(out, "vocab", [(i, i ^ bit) for i in range(size)])
        out = out + other
        bit *= 2
    return out


def make_body(ring):
    def on_device(hidden, head_weight, lengths, targets, policy_logprobs):
        row_count = hidden.shape[0]
        dp_size = lax.axis_size("dp")
        vocab_size = lax.axis_size("vocab")
        all_rows = row_count * dp_size
        slot_count = all_rows // MB
        tile_width = head_weight.shape[1]
        col_start = lax.axis_index("dp") * tile_width
        full_rows = ring_gather(hidden, ring)
        partial = jnp.dot(full_rows, head_weight, preferred_element_type=jnp.float32)
        logits, first = halving_scatter(partial, vocab_size)
        share = logits.shape[0]
        row_targets = lax.dynamic_slice_in_dim(targets, first, share)
        highest = jnp.max(logits, axis=1)
        exp_total = jnp.sum(jnp.exp(logits - highest[:, None]), axis=1)
        columns = col_start + lax.broadcasted_iota(jnp.int32, logits.shape, 1)
        picked = jnp.sum(jnp.where(columns == row_targets[:, None], logits, 0.0), axis=1)
        stats = merge_stats(jnp.stack([highest, exp_total, picked]), dp_size)
        logprob = stats[2] - (stats[0] + jnp.log(stats[1]))
        all_values = doubling_gather(logprob, first, vocab_size)
        own_values = lax.dynamic_slice_in_dim(all_values, lax.axis_index("dp") * row_count, row_count)
        global_rows = lax.axis_index("dp") * row_count + jnp.arange(row_count, dtype=jnp.int32)
        batches = jnp.arange(MB, dtype=jnp.int32)
        member = (global_rows // slot_count)[:, None] == batches[None, :]
        in_batch = global_rows % slot_count
        is_live = in_batch < jnp.sum(jnp.where(member, lengths[None, :], 0), axis=1)
        ref_logprob = jnp.where(is_live, own_values, 0.0)
        ratio_log = jnp.clip(ref_logprob - policy_logprobs, -20.0, 20.0)
        kl_value = jnp.where(is_live, jnp.minimum(jnp.exp(ratio_log) - ratio_log - 1.0, 10.0), 0.0)
        return (ref_logprob, kl_value)

    return on_device


def solution(mesh):
    return jax.shard_map(
        make_body(dp_ring(mesh)),
        mesh=mesh,
        in_specs=(P("dp", "vocab"), P("vocab", "dp"), P(), P(), P("dp")),
        out_specs=(P("dp"), P("dp")),
        check_vma=False,
    )
```

```python
import numpy as np
import jax
import jax.numpy as jnp
from jax import lax
from jax.sharding import PartitionSpec as P

MB = 8


def dp_ring(mesh):
    size = mesh.shape["dp"]
    try:
        coords = [tuple(dev.coords) for dev in mesh.devices[:, 0]]
        xs = sorted({c[0] for c in coords})
        zs = sorted({c[2] for c in coords})
        if len(xs) * len(zs) != size or len(zs) % 2:
            raise ValueError
        where = {(c[0], c[2]): i for i, c in enumerate(coords)}
        order = [where[(xs[0], z)] for z in zs]
        for row, z in enumerate(reversed(zs)):
            cols = xs[1:] if row % 2 == 0 else list(reversed(xs[1:]))
            order += [where[(x, z)] for x in cols]
        if sorted(order) != list(range(size)):
            raise ValueError
        return order
    except Exception:
        return list(range(size))


def ring_gather(block, ring, rows):
    size = len(ring)
    pos_of = np.argsort(np.asarray(ring))
    fwd = [(ring[i], ring[(i + 1) % size]) for i in range(size)]
    bwd = [(ring[(i + 1) % size], ring[i]) for i in range(size)]
    slots = [None] * size
    slots[0] = block
    ahead, behind = block, block
    for step in range(1, size // 2 + 1):
        ahead = lax.ppermute(ahead, "dp", fwd)
        slots[step] = ahead
        if step < size - step:
            behind = lax.ppermute(behind, "dp", bwd)
            slots[size - step] = behind
    count = block.shape[0]
    stacked = jnp.stack(slots).reshape(-1, block.shape[1])
    me = jnp.asarray(pos_of, jnp.int32)[lax.axis_index("dp")]
    slot_of = (me - jnp.asarray(pos_of, jnp.int32)) % size
    where = slot_of[rows // count] * count + rows % count
    return jnp.take(stacked, where, axis=0)


def halving_scatter(partial, size):
    me = lax.axis_index("vocab")
    first = jnp.int32(0)
    bit = 1
    while bit < size:
        half = partial.shape[0] // 2
        pairs = partial.reshape(2, half, partial.shape[1])
        side = (me // bit) % 2
        keep = jnp.take(pairs, side, axis=0)
        send = jnp.take(pairs, 1 - side, axis=0)
        got = lax.ppermute(send, "vocab", [(i, i ^ bit) for i in range(size)])
        partial = keep + got
        first = first + side * half
        bit *= 2
    return partial, first


def merge_stats(stats, size):
    bit = 1
    while bit < size:
        other = lax.ppermute(stats, "dp", [(i, i ^ bit) for i in range(size)])
        top = jnp.maximum(stats[0], other[0])
        total = stats[1] * jnp.exp(stats[0] - top) + other[1] * jnp.exp(other[0] - top)
        stats = jnp.stack([top, total, stats[2] + other[2]])
        bit *= 2
    return stats


def doubling_gather(values, first, size):
    me = lax.axis_index("vocab")
    total = values.shape[0] * size
    out = jnp.zeros((total,), values.dtype)
    out = lax.dynamic_update_slice(out, values, (first,))
    bit = 1
    while bit < size:
        other = lax.ppermute(out, "vocab", [(i, i ^ bit) for i in range(size)])
        out = out + other
        bit *= 2
    return out


def make_body(ring):
    def on_device(hidden, head_weight, lengths, targets, policy_logprobs):
        row_count = hidden.shape[0]
        dp_size = lax.axis_size("dp")
        vocab_size = lax.axis_size("vocab")
        all_rows = row_count * dp_size
        slot_count = all_rows // MB
        tile_width = head_weight.shape[1]
        col_start = lax.axis_index("dp") * tile_width
        global_ids = jnp.arange(all_rows, dtype=jnp.int32)
        lives = jnp.take(lengths, global_ids // slot_count)
        live_all = (global_ids % slot_count) < lives
        live_count = all_rows * 5 // 8
        upto = jnp.cumsum(live_all.astype(jnp.int32))
        packed = jnp.arange(live_count, dtype=jnp.int32)
        live_rows = jnp.sum((upto[None, :] <= packed[:, None]).astype(jnp.int32), axis=1)
        full_rows = ring_gather(hidden, ring, live_rows)
        partial = jnp.dot(full_rows, head_weight, preferred_element_type=jnp.float32)
        logits, first = halving_scatter(partial, vocab_size)
        share = logits.shape[0]
        row_targets = jnp.take(targets, lax.dynamic_slice_in_dim(live_rows, first, share))
        highest = jnp.max(logits, axis=1)
        exp_total = jnp.sum(jnp.exp(logits - highest[:, None]), axis=1)
        columns = col_start + lax.broadcasted_iota(jnp.int32, logits.shape, 1)
        picked = jnp.sum(jnp.where(columns == row_targets[:, None], logits, 0.0), axis=1)
        stats = merge_stats(jnp.stack([highest, exp_total, picked]), dp_size)
        logprob = stats[2] - (stats[0] + jnp.log(stats[1]))
        all_values = doubling_gather(logprob, first, vocab_size)
        is_live = lax.dynamic_slice_in_dim(live_all, lax.axis_index("dp") * row_count, row_count)
        own_slot = jnp.clip(lax.dynamic_slice_in_dim(upto, lax.axis_index("dp") * row_count, row_count) - 1, 0, live_count - 1)
        own_values = jnp.take(all_values, own_slot)
        ref_logprob = jnp.where(is_live, own_values, 0.0)
        ratio_log = jnp.clip(ref_logprob - policy_logprobs, -20.0, 20.0)
        kl_value = jnp.where(is_live, jnp.minimum(jnp.exp(ratio_log) - ratio_log - 1.0, 10.0), 0.0)
        return (ref_logprob, kl_value)

    return on_device


def solution(mesh):
    return jax.shard_map(
        make_body(dp_ring(mesh)),
        mesh=mesh,
        in_specs=(P("dp", "vocab"), P("vocab", "dp"), P(), P(), P("dp")),
        out_specs=(P("dp"), P("dp")),
        check_vma=False,
    )
```

```python
import numpy as np
import jax
import jax.numpy as jnp
from jax import lax
from jax.sharding import PartitionSpec as P

MB = 8


def dp_ring(mesh):
    size = mesh.shape["dp"]
    try:
        coords = [tuple(dev.coords) for dev in mesh.devices[:, 0]]
        xs = sorted({c[0] for c in coords})
        zs = sorted({c[2] for c in coords})
        if len(xs) * len(zs) != size or len(zs) % 2:
            raise ValueError
        where = {(c[0], c[2]): i for i, c in enumerate(coords)}
        order = [where[(xs[0], z)] for z in zs]
        for row, z in enumerate(reversed(zs)):
            cols = xs[1:] if row % 2 == 0 else list(reversed(xs[1:]))
            order += [where[(x, z)] for x in cols]
        if sorted(order) != list(range(size)):
            raise ValueError
        return order
    except Exception:
        return list(range(size))


def ring_gather(block, ring, rows):
    size = len(ring)
    pos_of = np.argsort(np.asarray(ring))
    fwd = [(ring[i], ring[(i + 1) % size]) for i in range(size)]
    bwd = [(ring[(i + 1) % size], ring[i]) for i in range(size)]
    slots = [None] * size
    slots[0] = block
    ahead, behind = block, block
    for step in range(1, size // 2 + 1):
        ahead = lax.ppermute(ahead, "dp", fwd)
        slots[step] = ahead
        if step < size - step:
            behind = lax.ppermute(behind, "dp", bwd)
            slots[size - step] = behind
    count = block.shape[0]
    stacked = jnp.stack(slots).reshape(-1, block.shape[1])
    me = jnp.asarray(pos_of, jnp.int32)[lax.axis_index("dp")]
    slot_of = (me - jnp.asarray(pos_of, jnp.int32)) % size
    where = slot_of[rows // count] * count + rows % count
    return jnp.take(stacked, where, axis=0)


def halving_scatter(partial, size):
    me = lax.axis_index("vocab")
    first = jnp.int32(0)
    bit = 1
    while bit < size:
        half = partial.shape[0] // 2
        pairs = partial.reshape(2, half, partial.shape[1])
        side = (me // bit) % 2
        keep = jnp.take(pairs, side, axis=0)
        send = jnp.take(pairs, 1 - side, axis=0)
        got = lax.ppermute(send, "vocab", [(i, i ^ bit) for i in range(size)])
        partial = keep + got
        first = first + side * half
        bit *= 2
    return partial, first


def merge_stats(stats, size):
    bit = 1
    while bit < size:
        other = lax.ppermute(stats, "dp", [(i, i ^ bit) for i in range(size)])
        top = jnp.maximum(stats[0], other[0])
        total = stats[1] * jnp.exp(stats[0] - top) + other[1] * jnp.exp(other[0] - top)
        stats = jnp.stack([top, total, stats[2] + other[2]])
        bit *= 2
    return stats


def doubling_gather(values, first, size):
    me = lax.axis_index("vocab")
    total = values.shape[0] * size
    out = jnp.zeros((total,), values.dtype)
    out = lax.dynamic_update_slice(out, values, (first,))
    bit = 1
    while bit < size:
        other = lax.ppermute(out, "vocab", [(i, i ^ bit) for i in range(size)])
        out = out + other
        bit *= 2
    return out


def make_body(ring):
    def on_device(hidden, head_weight, lengths, targets, policy_logprobs):
        row_count = hidden.shape[0]
        dp_size = lax.axis_size("dp")
        vocab_size = lax.axis_size("vocab")
        all_rows = row_count * dp_size
        slot_count = all_rows // MB
        tile_width = head_weight.shape[1]
        col_start = lax.axis_index("dp") * tile_width
        live_count = all_rows * 5 // 8
        ends = jnp.cumsum(lengths)
        starts = ends - lengths
        packed = jnp.arange(live_count, dtype=jnp.int32)
        batch_of = jnp.sum((ends[None, :] <= packed[:, None]).astype(jnp.int32), axis=1)
        live_rows = batch_of * slot_count + packed - jnp.take(starts, batch_of)
        full_rows = ring_gather(hidden, ring, live_rows)
        partial = jnp.dot(full_rows, head_weight, preferred_element_type=jnp.float32)
        logits, first = halving_scatter(partial, vocab_size)
        share = logits.shape[0]
        row_targets = jnp.take(targets, lax.dynamic_slice_in_dim(live_rows, first, share))
        highest = jnp.max(logits, axis=1)
        exp_total = jnp.sum(jnp.exp(logits - highest[:, None]), axis=1)
        columns = col_start + lax.broadcasted_iota(jnp.int32, logits.shape, 1)
        picked = jnp.sum(jnp.where(columns == row_targets[:, None], logits, 0.0), axis=1)
        stats = merge_stats(jnp.stack([highest, exp_total, picked]), dp_size)
        logprob = stats[2] - (stats[0] + jnp.log(stats[1]))
        all_values = doubling_gather(logprob, first, vocab_size)
        own_rows = lax.axis_index("dp") * row_count + jnp.arange(row_count, dtype=jnp.int32)
        own_batch = own_rows // slot_count
        is_live = own_rows % slot_count < jnp.take(lengths, own_batch)
        own_slot = jnp.clip(jnp.take(starts, own_batch) + own_rows % slot_count, 0, live_count - 1)
        own_values = jnp.take(all_values, own_slot)
        ref_logprob = jnp.where(is_live, own_values, 0.0)
        ratio_log = jnp.clip(ref_logprob - policy_logprobs, -20.0, 20.0)
        kl_value = jnp.where(is_live, jnp.minimum(jnp.exp(ratio_log) - ratio_log - 1.0, 10.0), 0.0)
        return (ref_logprob, kl_value)

    return on_device


def solution(mesh):
    return jax.shard_map(
        make_body(dp_ring(mesh)),
        mesh=mesh,
        in_specs=(P("dp", "vocab"), P("vocab", "dp"), P(), P(), P("dp")),
        out_specs=(P("dp"), P("dp")),
        check_vma=False,
    )
```

```python
import numpy as np
import jax
import jax.numpy as jnp
from jax import lax
from jax.sharding import PartitionSpec as P

MB = 8


def dp_ring(mesh):
    size = mesh.shape["dp"]
    try:
        coords = [tuple(dev.coords) for dev in mesh.devices[:, 0]]
        xs = sorted({c[0] for c in coords})
        zs = sorted({c[2] for c in coords})
        if len(xs) * len(zs) != size or len(zs) % 2:
            raise ValueError
        where = {(c[0], c[2]): i for i, c in enumerate(coords)}
        order = [where[(xs[0], z)] for z in zs]
        for row, z in enumerate(reversed(zs)):
            cols = xs[1:] if row % 2 == 0 else list(reversed(xs[1:]))
            order += [where[(x, z)] for x in cols]
        if sorted(order) != list(range(size)):
            raise ValueError
        return order
    except Exception:
        return list(range(size))


def ring_gather(block, ring, rows):
    size = len(ring)
    pos_of = np.argsort(np.asarray(ring))
    fwd = [(ring[i], ring[(i + 1) % size]) for i in range(size)]
    bwd = [(ring[(i + 1) % size], ring[i]) for i in range(size)]
    slots = [None] * size
    slots[0] = block
    ahead, behind = block, block
    for step in range(1, size // 2 + 1):
        ahead = lax.ppermute(ahead, "dp", fwd)
        slots[step] = ahead
        if step < size - step:
            behind = lax.ppermute(behind, "dp", bwd)
            slots[size - step] = behind
    count = block.shape[0]
    stacked = jnp.stack(slots).reshape(-1, block.shape[1])
    me = jnp.asarray(pos_of, jnp.int32)[lax.axis_index("dp")]
    slot_of = (me - jnp.asarray(pos_of, jnp.int32)) % size
    owner = rows // count
    hit = owner[None, :] == jnp.arange(size, dtype=jnp.int32)[:, None]
    where = jnp.sum(jnp.where(hit, slot_of[:, None], 0), axis=0) * count + rows % count
    choose = lax.broadcasted_iota(jnp.int32, (stacked.shape[0], where.shape[0]), 0) == where[None, :]
    picked = lax.dot_general(choose.astype(stacked.dtype), stacked, (((0,), (0,)), ((), ())), preferred_element_type=jnp.float32)
    return picked.astype(stacked.dtype)


def halving_scatter(partial, size):
    me = lax.axis_index("vocab")
    first = jnp.int32(0)
    bit = 1
    while bit < size:
        half = partial.shape[0] // 2
        pairs = partial.reshape(2, half, partial.shape[1])
        side = (me // bit) % 2
        keep = jnp.take(pairs, side, axis=0)
        send = jnp.take(pairs, 1 - side, axis=0)
        got = lax.ppermute(send, "vocab", [(i, i ^ bit) for i in range(size)])
        partial = keep + got
        first = first + side * half
        bit *= 2
    return partial, first


def merge_stats(stats, size):
    bit = 1
    while bit < size:
        other = lax.ppermute(stats, "dp", [(i, i ^ bit) for i in range(size)])
        top = jnp.maximum(stats[0], other[0])
        total = stats[1] * jnp.exp(stats[0] - top) + other[1] * jnp.exp(other[0] - top)
        stats = jnp.stack([top, total, stats[2] + other[2]])
        bit *= 2
    return stats


def doubling_gather(values, first, size):
    me = lax.axis_index("vocab")
    total = values.shape[0] * size
    out = jnp.zeros((total,), values.dtype)
    out = lax.dynamic_update_slice(out, values, (first,))
    bit = 1
    while bit < size:
        other = lax.ppermute(out, "vocab", [(i, i ^ bit) for i in range(size)])
        out = out + other
        bit *= 2
    return out


def make_body(ring):
    def on_device(hidden, head_weight, lengths, targets, policy_logprobs):
        row_count = hidden.shape[0]
        dp_size = lax.axis_size("dp")
        vocab_size = lax.axis_size("vocab")
        all_rows = row_count * dp_size
        slot_count = all_rows // MB
        tile_width = head_weight.shape[1]
        col_start = lax.axis_index("dp") * tile_width
        live_count = all_rows * 5 // 8
        ends = jnp.cumsum(lengths)
        starts = ends - lengths
        packed = jnp.arange(live_count, dtype=jnp.int32)
        batch_hit = ends[:, None] <= packed[None, :]
        batch_of = jnp.sum(batch_hit.astype(jnp.int32), axis=0)
        in_batch = packed - jnp.sum(jnp.where(batch_of[None, :] == jnp.arange(MB, dtype=jnp.int32)[:, None], starts[:, None], 0), axis=0)
        live_rows = batch_of * slot_count + in_batch
        full_rows = ring_gather(hidden, ring, live_rows)
        partial = jnp.dot(full_rows, head_weight, preferred_element_type=jnp.float32)
        logits, first = halving_scatter(partial, vocab_size)
        share = logits.shape[0]
        row_targets = jnp.take(targets, lax.dynamic_slice_in_dim(live_rows, first, share))
        highest = jnp.max(logits, axis=1)
        exp_total = jnp.sum(jnp.exp(logits - highest[:, None]), axis=1)
        columns = col_start + lax.broadcasted_iota(jnp.int32, logits.shape, 1)
        picked = jnp.sum(jnp.where(columns == row_targets[:, None], logits, 0.0), axis=1)
        stats = merge_stats(jnp.stack([highest, exp_total, picked]), dp_size)
        logprob = stats[2] - (stats[0] + jnp.log(stats[1]))
        all_values = doubling_gather(logprob, first, vocab_size)
        own_rows = lax.axis_index("dp") * row_count + jnp.arange(row_count, dtype=jnp.int32)
        own_batch = own_rows // slot_count
        is_live = own_rows % slot_count < jnp.take(lengths, own_batch)
        own_slot = jnp.clip(jnp.take(starts, own_batch) + own_rows % slot_count, 0, live_count - 1)
        own_values = jnp.take(all_values, own_slot)
        ref_logprob = jnp.where(is_live, own_values, 0.0)
        ratio_log = jnp.clip(ref_logprob - policy_logprobs, -20.0, 20.0)
        kl_value = jnp.where(is_live, jnp.minimum(jnp.exp(ratio_log) - ratio_log - 1.0, 10.0), 0.0)
        return (ref_logprob, kl_value)

    return on_device


def solution(mesh):
    return jax.shard_map(
        make_body(dp_ring(mesh)),
        mesh=mesh,
        in_specs=(P("dp", "vocab"), P("vocab", "dp"), P(), P(), P("dp")),
        out_specs=(P("dp"), P("dp")),
        check_vma=False,
    )
```

```python
import numpy as np
import jax
import jax.numpy as jnp
from jax import lax
from jax.sharding import PartitionSpec as P

MB = 8


def dp_ring(mesh):
    size = mesh.shape["dp"]
    try:
        coords = [tuple(dev.coords) for dev in mesh.devices[:, 0]]
        xs = sorted({c[0] for c in coords})
        zs = sorted({c[2] for c in coords})
        if len(xs) * len(zs) != size or len(zs) % 2:
            raise ValueError
        where = {(c[0], c[2]): i for i, c in enumerate(coords)}
        order = [where[(xs[0], z)] for z in zs]
        for row, z in enumerate(reversed(zs)):
            cols = xs[1:] if row % 2 == 0 else list(reversed(xs[1:]))
            order += [where[(x, z)] for x in cols]
        if sorted(order) != list(range(size)):
            raise ValueError
        return order
    except Exception:
        return list(range(size))


def ring_gather(block, ring, rows):
    size = len(ring)
    pos_of = np.argsort(np.asarray(ring))
    fwd = [(ring[i], ring[(i + 1) % size]) for i in range(size)]
    bwd = [(ring[(i + 1) % size], ring[i]) for i in range(size)]
    slots = [None] * size
    slots[0] = block
    ahead, behind = block, block
    for step in range(1, size // 2 + 1):
        ahead = lax.ppermute(ahead, "dp", fwd)
        slots[step] = ahead
        if step < size - step:
            behind = lax.ppermute(behind, "dp", bwd)
            slots[size - step] = behind
    count = block.shape[0]
    stacked = jnp.stack(slots).reshape(-1, block.shape[1])
    me = jnp.asarray(pos_of, jnp.int32)[lax.axis_index("dp")]
    slot_of = (me - jnp.asarray(pos_of, jnp.int32)) % size
    owner = rows // count
    hit = owner[None, :] == jnp.arange(size, dtype=jnp.int32)[:, None]
    where = jnp.sum(jnp.where(hit, slot_of[:, None], 0), axis=0) * count + rows % count
    choose = lax.broadcasted_iota(jnp.int32, (stacked.shape[0], where.shape[0]), 0) == where[None, :]
    picked = lax.dot_general(choose.astype(stacked.dtype), stacked, (((0,), (0,)), ((), ())), preferred_element_type=jnp.float32)
    return picked.astype(stacked.dtype)


def halving_scatter(partial, size):
    bit = 1
    while bit < size:
        half = partial.shape[0] // 2
        got = lax.ppermute(partial[:half], "vocab", [(i, i ^ bit) for i in range(size)])
        partial = partial[half:] + got
        bit *= 2
    return partial


def send_first_order(count, size):
    me = lax.axis_index("vocab")
    place = jnp.arange(count, dtype=jnp.int32)
    canon = jnp.zeros((count,), jnp.int32)
    first = jnp.int32(0)
    span, bit, level = count, 1, 0
    while bit < size:
        span //= 2
        side = (me // bit) % 2
        digit = (place // span) % 2
        canon = canon + ((1 - side) ^ digit) * span
        first = first + side * span
        bit *= 2
        level += 1
    return canon + place % span, first


def merge_stats(stats, size):
    bit = 1
    while bit < size:
        other = lax.ppermute(stats, "dp", [(i, i ^ bit) for i in range(size)])
        top = jnp.maximum(stats[0], other[0])
        total = stats[1] * jnp.exp(stats[0] - top) + other[1] * jnp.exp(other[0] - top)
        stats = jnp.stack([top, total, stats[2] + other[2]])
        bit *= 2
    return stats


def doubling_gather(values, first, size):
    me = lax.axis_index("vocab")
    total = values.shape[0] * size
    out = jnp.zeros((total,), values.dtype)
    out = lax.dynamic_update_slice(out, values, (first,))
    bit = 1
    while bit < size:
        other = lax.ppermute(out, "vocab", [(i, i ^ bit) for i in range(size)])
        out = out + other
        bit *= 2
    return out


def make_body(ring):
    def on_device(hidden, head_weight, lengths, targets, policy_logprobs):
        row_count = hidden.shape[0]
        dp_size = lax.axis_size("dp")
        vocab_size = lax.axis_size("vocab")
        all_rows = row_count * dp_size
        slot_count = all_rows // MB
        tile_width = head_weight.shape[1]
        col_start = lax.axis_index("dp") * tile_width
        live_count = all_rows * 5 // 8
        ends = jnp.cumsum(lengths)
        starts = ends - lengths
        packed, first = send_first_order(live_count, vocab_size)
        batch_hit = ends[:, None] <= packed[None, :]
        batch_of = jnp.sum(batch_hit.astype(jnp.int32), axis=0)
        in_batch = packed - jnp.sum(jnp.where(batch_of[None, :] == jnp.arange(MB, dtype=jnp.int32)[:, None], starts[:, None], 0), axis=0)
        live_rows = batch_of * slot_count + in_batch
        full_rows = ring_gather(hidden, ring, live_rows)
        share = live_count // vocab_size
        row_targets = lax.dynamic_slice_in_dim(live_rows, live_count - share, share)
        row_targets = jnp.take(targets, row_targets)
        pieces = 2 if tile_width % 256 == 0 else 1
        width = tile_width // pieces
        parts = []
        for piece in range(pieces):
            partial = jnp.dot(full_rows, head_weight[:, piece * width:(piece + 1) * width], preferred_element_type=jnp.float32)
            logits = halving_scatter(partial, vocab_size)
            highest = jnp.max(logits, axis=1)
            exp_total = jnp.sum(jnp.exp(logits - highest[:, None]), axis=1)
            columns = col_start + piece * width + lax.broadcasted_iota(jnp.int32, logits.shape, 1)
            picked = jnp.sum(jnp.where(columns == row_targets[:, None], logits, 0.0), axis=1)
            parts.append((highest, exp_total, picked))
        highest = parts[0][0]
        for part in parts[1:]:
            highest = jnp.maximum(highest, part[0])
        exp_total = sum(part[1] * jnp.exp(part[0] - highest) for part in parts)
        picked = sum(part[2] for part in parts)
        stats = merge_stats(jnp.stack([highest, exp_total, picked]), dp_size)
        logprob = stats[2] - (stats[0] + jnp.log(stats[1]))
        all_values = doubling_gather(logprob, first, vocab_size)
        own_rows = lax.axis_index("dp") * row_count + jnp.arange(row_count, dtype=jnp.int32)
        own_batch = own_rows // slot_count
        is_live = own_rows % slot_count < jnp.take(lengths, own_batch)
        own_slot = jnp.clip(jnp.take(starts, own_batch) + own_rows % slot_count, 0, live_count - 1)
        own_values = jnp.take(all_values, own_slot)
        ref_logprob = jnp.where(is_live, own_values, 0.0)
        ratio_log = jnp.clip(ref_logprob - policy_logprobs, -20.0, 20.0)
        kl_value = jnp.where(is_live, jnp.minimum(jnp.exp(ratio_log) - ratio_log - 1.0, 10.0), 0.0)
        return (ref_logprob, kl_value)

    return on_device


def solution(mesh):
    return jax.shard_map(
        make_body(dp_ring(mesh)),
        mesh=mesh,
        in_specs=(P("dp", "vocab"), P("vocab", "dp"), P(), P(), P("dp")),
        out_specs=(P("dp"), P("dp")),
        check_vma=False,
    )
```

```python
import numpy as np
import jax
import jax.numpy as jnp
from jax import lax
from jax.sharding import PartitionSpec as P

MB = 8


def dp_ring(mesh):
    size = mesh.shape["dp"]
    try:
        coords = [tuple(dev.coords) for dev in mesh.devices[:, 0]]
        xs = sorted({c[0] for c in coords})
        zs = sorted({c[2] for c in coords})
        if len(xs) * len(zs) != size or len(zs) % 2:
            raise ValueError
        where = {(c[0], c[2]): i for i, c in enumerate(coords)}
        order = [where[(xs[0], z)] for z in zs]
        for row, z in enumerate(reversed(zs)):
            cols = xs[1:] if row % 2 == 0 else list(reversed(xs[1:]))
            order += [where[(x, z)] for x in cols]
        if sorted(order) != list(range(size)):
            raise ValueError
        return order
    except Exception:
        return list(range(size))


def ring_gather(block, ring, rows):
    size = len(ring)
    pos_of = np.argsort(np.asarray(ring))
    fwd = [(ring[i], ring[(i + 1) % size]) for i in range(size)]
    bwd = [(ring[(i + 1) % size], ring[i]) for i in range(size)]
    slots = [None] * size
    slots[0] = block
    ahead, behind = block, block
    for step in range(1, size // 2 + 1):
        ahead = lax.ppermute(ahead, "dp", fwd)
        slots[step] = ahead
        if step < size - step:
            behind = lax.ppermute(behind, "dp", bwd)
            slots[size - step] = behind
    count = block.shape[0]
    stacked = jnp.stack(slots).reshape(-1, block.shape[1])
    me = jnp.asarray(pos_of, jnp.int32)[lax.axis_index("dp")]
    slot_of = (me - jnp.asarray(pos_of, jnp.int32)) % size
    owner = rows // count
    hit = owner[None, :] == jnp.arange(size, dtype=jnp.int32)[:, None]
    where = jnp.sum(jnp.where(hit, slot_of[:, None], 0), axis=0) * count + rows % count
    choose = lax.broadcasted_iota(jnp.int32, (stacked.shape[0], where.shape[0]), 0) == where[None, :]
    picked = lax.dot_general(choose.astype(stacked.dtype), stacked, (((0,), (0,)), ((), ())), preferred_element_type=jnp.float32)
    return picked.astype(stacked.dtype)


def halving_scatter(partial, size):
    bit = 1
    while bit < size:
        half = partial.shape[0] // 2
        got = lax.ppermute(partial[:half], "vocab", [(i, i ^ bit) for i in range(size)])
        partial = partial[half:] + got
        bit *= 2
    return partial


def send_first_order(count, size):
    me = lax.axis_index("vocab")
    place = jnp.arange(count, dtype=jnp.int32)
    canon = jnp.zeros((count,), jnp.int32)
    first = jnp.int32(0)
    span, bit, level = count, 1, 0
    while bit < size:
        span //= 2
        side = (me // bit) % 2
        digit = (place // span) % 2
        canon = canon + ((1 - side) ^ digit) * span
        first = first + side * span
        bit *= 2
        level += 1
    return canon + place % span, first


def merge_stats(stats, size):
    bit = 1
    while bit < size:
        other = lax.ppermute(stats, "dp", [(i, i ^ bit) for i in range(size)])
        top = jnp.maximum(stats[0], other[0])
        total = stats[1] * jnp.exp(stats[0] - top) + other[1] * jnp.exp(other[0] - top)
        stats = jnp.stack([top, total, stats[2] + other[2]])
        bit *= 2
    return stats


def doubling_gather(values, first, size):
    me = lax.axis_index("vocab")
    total = values.shape[0] * size
    out = jnp.zeros((total,), values.dtype)
    out = lax.dynamic_update_slice(out, values, (first,))
    bit = 1
    while bit < size:
        other = lax.ppermute(out, "vocab", [(i, i ^ bit) for i in range(size)])
        out = out + other
        bit *= 2
    return out


def make_body(ring):
    def on_device(hidden, head_weight, lengths, targets, policy_logprobs):
        row_count = hidden.shape[0]
        dp_size = lax.axis_size("dp")
        vocab_size = lax.axis_size("vocab")
        all_rows = row_count * dp_size
        slot_count = all_rows // MB
        tile_width = head_weight.shape[1]
        col_start = lax.axis_index("dp") * tile_width
        live_count = all_rows * 5 // 8
        ends = jnp.cumsum(lengths)
        starts = ends - lengths
        packed, first = send_first_order(live_count, vocab_size)
        batch_hit = ends[:, None] <= packed[None, :]
        batch_of = jnp.sum(batch_hit.astype(jnp.int32), axis=0)
        in_batch = packed - jnp.sum(jnp.where(batch_of[None, :] == jnp.arange(MB, dtype=jnp.int32)[:, None], starts[:, None], 0), axis=0)
        live_rows = batch_of * slot_count + in_batch
        full_rows = ring_gather(hidden, ring, live_rows)
        share = live_count // vocab_size
        row_targets = lax.dynamic_slice_in_dim(live_rows, live_count - share, share)
        row_targets = jnp.take(targets, row_targets)
        tail = tile_width // 4 if tile_width % 512 == 0 else 0
        bounds = [(0, tile_width - tail), (tile_width - tail, tile_width)] if tail else [(0, tile_width)]
        merged = []
        for low, high in bounds:
            partial = jnp.dot(full_rows, head_weight[:, low:high], preferred_element_type=jnp.float32)
            partial, full_rows = lax.optimization_barrier((partial, full_rows))
            logits = halving_scatter(partial, vocab_size)
            highest = jnp.max(logits, axis=1)
            exp_total = jnp.sum(jnp.exp(logits - highest[:, None]), axis=1)
            columns = col_start + low + lax.broadcasted_iota(jnp.int32, logits.shape, 1)
            picked = jnp.sum(jnp.where(columns == row_targets[:, None], logits, 0.0), axis=1)
            merged.append(merge_stats(jnp.stack([highest, exp_total, picked]), dp_size))
        top = merged[0][0]
        for part in merged[1:]:
            top = jnp.maximum(top, part[0])
        stats = jnp.stack([top, sum(part[1] * jnp.exp(part[0] - top) for part in merged), sum(part[2] for part in merged)])
        logprob = stats[2] - (stats[0] + jnp.log(stats[1]))
        all_values = doubling_gather(logprob, first, vocab_size)
        own_rows = lax.axis_index("dp") * row_count + jnp.arange(row_count, dtype=jnp.int32)
        own_batch = own_rows // slot_count
        is_live = own_rows % slot_count < jnp.take(lengths, own_batch)
        own_slot = jnp.clip(jnp.take(starts, own_batch) + own_rows % slot_count, 0, live_count - 1)
        own_values = jnp.take(all_values, own_slot)
        ref_logprob = jnp.where(is_live, own_values, 0.0)
        ratio_log = jnp.clip(ref_logprob - policy_logprobs, -20.0, 20.0)
        kl_value = jnp.where(is_live, jnp.minimum(jnp.exp(ratio_log) - ratio_log - 1.0, 10.0), 0.0)
        return (ref_logprob, kl_value)

    return on_device


def solution(mesh):
    return jax.shard_map(
        make_body(dp_ring(mesh)),
        mesh=mesh,
        in_specs=(P("dp", "vocab"), P("vocab", "dp"), P(), P(), P("dp")),
        out_specs=(P("dp"), P("dp")),
        check_vma=False,
    )
```

```python
import numpy as np
import jax
import jax.numpy as jnp
from jax import lax
from jax.sharding import PartitionSpec as P

MB = 8


def dp_ring(mesh):
    size = mesh.shape["dp"]
    try:
        coords = [tuple(dev.coords) for dev in mesh.devices[:, 0]]
        xs = sorted({c[0] for c in coords})
        zs = sorted({c[2] for c in coords})
        if len(xs) * len(zs) != size or len(zs) % 2:
            raise ValueError
        where = {(c[0], c[2]): i for i, c in enumerate(coords)}
        order = [where[(xs[0], z)] for z in zs]
        for row, z in enumerate(reversed(zs)):
            cols = xs[1:] if row % 2 == 0 else list(reversed(xs[1:]))
            order += [where[(x, z)] for x in cols]
        if sorted(order) != list(range(size)):
            raise ValueError
        return order
    except Exception:
        return list(range(size))


def ring_gather(block, ring, rows):
    size = len(ring)
    pos_of = np.argsort(np.asarray(ring))
    fwd = [(ring[i], ring[(i + 1) % size]) for i in range(size)]
    bwd = [(ring[(i + 1) % size], ring[i]) for i in range(size)]
    slots = [None] * size
    slots[0] = block
    ahead, behind = block, block
    for step in range(1, size // 2 + 1):
        ahead = lax.ppermute(ahead, "dp", fwd)
        slots[step] = ahead
        if step < size - step:
            behind = lax.ppermute(behind, "dp", bwd)
            slots[size - step] = behind
    count = block.shape[0]
    stacked = jnp.stack(slots).reshape(-1, block.shape[1])
    me = jnp.asarray(pos_of, jnp.int32)[lax.axis_index("dp")]
    slot_of = (me - jnp.asarray(pos_of, jnp.int32)) % size
    owner = rows // count
    hit = owner[None, :] == jnp.arange(size, dtype=jnp.int32)[:, None]
    where = jnp.sum(jnp.where(hit, slot_of[:, None], 0), axis=0) * count + rows % count
    choose = lax.broadcasted_iota(jnp.int32, (stacked.shape[0], where.shape[0]), 0) == where[None, :]
    picked = lax.dot_general(choose.astype(stacked.dtype), stacked, (((0,), (0,)), ((), ())), preferred_element_type=jnp.float32)
    return lax.optimization_barrier(picked.astype(stacked.dtype))


def halving_scatter(partial, size):
    me = lax.axis_index("vocab")
    first = jnp.int32(0)
    bit = 1
    while bit < size:
        half = partial.shape[0] // 2
        pairs = partial.reshape(2, half, partial.shape[1])
        side = (me // bit) % 2
        keep = jnp.take(pairs, side, axis=0)
        send = jnp.take(pairs, 1 - side, axis=0)
        got = lax.ppermute(send, "vocab", [(i, i ^ bit) for i in range(size)])
        partial = keep + got
        first = first + side * half
        bit *= 2
    return partial, first


def merge_pair(stats, other):
    top = jnp.maximum(stats[0], other[0])
    total = stats[1] * jnp.exp(stats[0] - top) + other[1] * jnp.exp(other[0] - top)
    return jnp.stack([top, total, stats[2] + other[2]])


def merge_stats(stats, size):
    bit = 1
    while bit < size:
        if bit * 4 <= size:
            got = [lax.ppermute(stats, "dp", [(i, i ^ (bit * k)) for i in range(size)]) for k in (1, 2, 3)]
            stats = merge_pair(merge_pair(stats, got[0]), merge_pair(got[1], got[2]))
            bit *= 4
        else:
            stats = merge_pair(stats, lax.ppermute(stats, "dp", [(i, i ^ bit) for i in range(size)]))
            bit *= 2
    return stats


def doubling_gather(values, first, size):
    me = lax.axis_index("vocab")
    total = values.shape[0] * size
    out = jnp.zeros((total,), values.dtype)
    out = lax.dynamic_update_slice(out, values, (first,))
    bit = 1
    while bit < size:
        other = lax.ppermute(out, "vocab", [(i, i ^ bit) for i in range(size)])
        out = out + other
        bit *= 2
    return out


def make_body(ring):
    def on_device(hidden, head_weight, lengths, targets, policy_logprobs):
        row_count = hidden.shape[0]
        dp_size = lax.axis_size("dp")
        vocab_size = lax.axis_size("vocab")
        all_rows = row_count * dp_size
        slot_count = all_rows // MB
        tile_width = head_weight.shape[1]
        col_start = lax.axis_index("dp") * tile_width
        live_count = all_rows * 5 // 8
        ends = jnp.cumsum(lengths)
        starts = ends - lengths
        packed = jnp.arange(live_count, dtype=jnp.int32)
        batch_hit = ends[:, None] <= packed[None, :]
        batch_of = jnp.sum(batch_hit.astype(jnp.int32), axis=0)
        in_batch = packed - jnp.sum(jnp.where(batch_of[None, :] == jnp.arange(MB, dtype=jnp.int32)[:, None], starts[:, None], 0), axis=0)
        live_rows = batch_of * slot_count + in_batch
        full_rows = ring_gather(hidden, ring, live_rows)
        partial = jnp.dot(full_rows, head_weight, preferred_element_type=jnp.float32)
        logits, first = halving_scatter(partial, vocab_size)
        share = logits.shape[0]
        row_targets = jnp.take(targets, lax.dynamic_slice_in_dim(live_rows, first, share))
        highest = jnp.max(logits, axis=1)
        exp_total = jnp.sum(jnp.exp(logits - highest[:, None]), axis=1)
        columns = col_start + lax.broadcasted_iota(jnp.int32, logits.shape, 1)
        picked = jnp.sum(jnp.where(columns == row_targets[:, None], logits, 0.0), axis=1)
        stats = merge_stats(jnp.stack([highest, exp_total, picked]), dp_size)
        logprob = stats[2] - (stats[0] + jnp.log(stats[1]))
        all_values = doubling_gather(logprob, first, vocab_size)
        own_rows = lax.axis_index("dp") * row_count + jnp.arange(row_count, dtype=jnp.int32)
        own_batch = own_rows // slot_count
        is_live = own_rows % slot_count < jnp.take(lengths, own_batch)
        own_slot = jnp.clip(jnp.take(starts, own_batch) + own_rows % slot_count, 0, live_count - 1)
        own_values = jnp.take(all_values, own_slot)
        ref_logprob = jnp.where(is_live, own_values, 0.0)
        ratio_log = jnp.clip(ref_logprob - policy_logprobs, -20.0, 20.0)
        kl_value = jnp.where(is_live, jnp.minimum(jnp.exp(ratio_log) - ratio_log - 1.0, 10.0), 0.0)
        return (ref_logprob, kl_value)

    return on_device


def solution(mesh):
    return jax.shard_map(
        make_body(dp_ring(mesh)),
        mesh=mesh,
        in_specs=(P("dp", "vocab"), P("vocab", "dp"), P(), P(), P("dp")),
        out_specs=(P("dp"), P("dp")),
        check_vma=False,
    )
```

```python
import numpy as np
import jax
import jax.numpy as jnp
from jax import lax
from jax.sharding import PartitionSpec as P

MB = 8


def dp_ring(mesh):
    size = mesh.shape["dp"]
    try:
        coords = [tuple(dev.coords) for dev in mesh.devices[:, 0]]
        xs = sorted({c[0] for c in coords})
        zs = sorted({c[2] for c in coords})
        if len(xs) * len(zs) != size or len(zs) % 2:
            raise ValueError
        where = {(c[0], c[2]): i for i, c in enumerate(coords)}
        order = [where[(xs[0], z)] for z in zs]
        for row, z in enumerate(reversed(zs)):
            cols = xs[1:] if row % 2 == 0 else list(reversed(xs[1:]))
            order += [where[(x, z)] for x in cols]
        if sorted(order) != list(range(size)):
            raise ValueError
        return order
    except Exception:
        return list(range(size))


def ring_gather(block, ring, rows):
    size = len(ring)
    pos_of = np.argsort(np.asarray(ring))
    fwd = [(ring[i], ring[(i + 1) % size]) for i in range(size)]
    bwd = [(ring[(i + 1) % size], ring[i]) for i in range(size)]
    slots = [None] * size
    slots[0] = block
    ahead, behind = block, block
    count = block.shape[0]
    for step in range(1, size // 2 + 1):
        if step == size - step and count % 32 == 0:
            front = lax.ppermute(ahead[:count // 2], "dp", fwd)
            back = lax.ppermute(behind[count // 2:], "dp", bwd)
            slots[step] = jnp.concatenate([front, back])
            continue
        ahead = lax.ppermute(ahead, "dp", fwd)
        slots[step] = ahead
        if step < size - step:
            behind = lax.ppermute(behind, "dp", bwd)
            slots[size - step] = behind
    count = block.shape[0]
    stacked = jnp.stack(slots).reshape(-1, block.shape[1])
    me = jnp.sum(jnp.where(jnp.arange(size) == lax.axis_index("dp"), jnp.asarray(pos_of, jnp.int32), 0))
    slot_of = (me - jnp.asarray(pos_of, jnp.int32)) % size
    owner = rows // count
    hit = owner[None, :] == jnp.arange(size, dtype=jnp.int32)[:, None]
    where = jnp.sum(jnp.where(hit, slot_of[:, None], 0), axis=0) * count + rows % count
    choose = lax.broadcasted_iota(jnp.int32, (stacked.shape[0], where.shape[0]), 0) == where[None, :]
    picked = lax.dot_general(choose.astype(stacked.dtype), stacked, (((0,), (0,)), ((), ())), preferred_element_type=jnp.float32)
    return lax.optimization_barrier(picked.astype(stacked.dtype))


def halving_scatter(partial, size):
    me = lax.axis_index("vocab")
    first = jnp.int32(0)
    bit = 1
    while bit < size:
        half = partial.shape[0] // 2
        pairs = partial.reshape(2, half, partial.shape[1])
        side = (me // bit) % 2
        keep = jnp.take(pairs, side, axis=0)
        send = jnp.take(pairs, 1 - side, axis=0)
        got = lax.ppermute(send, "vocab", [(i, i ^ bit) for i in range(size)])
        partial = keep + got
        first = first + side * half
        bit *= 2
    return partial, first


def merge_pair(stats, other):
    top = jnp.maximum(stats[0], other[0])
    total = stats[1] * jnp.exp(stats[0] - top) + other[1] * jnp.exp(other[0] - top)
    return jnp.stack([top, total, stats[2] + other[2]])


def merge_stats(stats, size):
    bit = 1
    while bit < size:
        if bit * 4 <= size:
            got = [lax.ppermute(stats, "dp", [(i, i ^ (bit * k)) for i in range(size)]) for k in (1, 2, 3)]
            stats = merge_pair(merge_pair(stats, got[0]), merge_pair(got[1], got[2]))
            bit *= 4
        else:
            stats = merge_pair(stats, lax.ppermute(stats, "dp", [(i, i ^ bit) for i in range(size)]))
            bit *= 2
    return stats


def doubling_gather(values, first, size):
    me = lax.axis_index("vocab")
    total = values.shape[0] * size
    out = jnp.zeros((total,), values.dtype)
    out = lax.dynamic_update_slice(out, values, (first,))
    bit = 1
    while bit < size:
        other = lax.ppermute(out, "vocab", [(i, i ^ bit) for i in range(size)])
        out = out + other
        bit *= 2
    return out


def make_body(ring):
    def on_device(hidden, head_weight, lengths, targets, policy_logprobs):
        row_count = hidden.shape[0]
        dp_size = lax.axis_size("dp")
        vocab_size = lax.axis_size("vocab")
        all_rows = row_count * dp_size
        slot_count = all_rows // MB
        tile_width = head_weight.shape[1]
        col_start = lax.axis_index("dp") * tile_width
        live_count = all_rows * 5 // 8
        ends = jnp.sum(jnp.where(jnp.arange(MB)[None, :] <= jnp.arange(MB)[:, None], lengths[None, :], 0), axis=1)
        starts = ends - lengths
        packed = jnp.arange(live_count, dtype=jnp.int32)
        batch_hit = ends[:, None] <= packed[None, :]
        batch_of = jnp.sum(batch_hit.astype(jnp.int32), axis=0)
        in_batch = packed - jnp.sum(jnp.where(batch_of[None, :] == jnp.arange(MB, dtype=jnp.int32)[:, None], starts[:, None], 0), axis=0)
        live_rows = batch_of * slot_count + in_batch
        full_rows = ring_gather(hidden, ring, live_rows)
        partial = jnp.dot(full_rows, head_weight, preferred_element_type=jnp.float32)
        logits, first = halving_scatter(partial, vocab_size)
        share = logits.shape[0]
        row_targets = jnp.take(targets, lax.dynamic_slice_in_dim(live_rows, first, share))
        highest = jnp.max(logits, axis=1)
        exp_total = jnp.sum(jnp.exp(logits - highest[:, None]), axis=1)
        columns = col_start + lax.broadcasted_iota(jnp.int32, logits.shape, 1)
        picked = jnp.sum(jnp.where(columns == row_targets[:, None], logits, 0.0), axis=1)
        stats = merge_stats(jnp.stack([highest, exp_total, picked]), dp_size)
        logprob = stats[2] - (stats[0] + jnp.log(stats[1]))
        all_values = doubling_gather(logprob, first, vocab_size)
        own_rows = lax.axis_index("dp") * row_count + jnp.arange(row_count, dtype=jnp.int32)
        if slot_count % row_count == 0:
            own_batch = lax.axis_index("dp") * row_count // slot_count
            hit = jnp.arange(MB) == own_batch
            own_length = jnp.sum(jnp.where(hit, lengths, 0))
            own_start = jnp.sum(jnp.where(hit, starts, 0))
            offset = lax.axis_index("dp") * row_count % slot_count
            is_live = offset + jnp.arange(row_count, dtype=jnp.int32) < own_length
            padded = jnp.concatenate([all_values, jnp.zeros((row_count,), all_values.dtype)])
            own_values = lax.dynamic_slice_in_dim(padded, jnp.clip(own_start + offset, 0, live_count), row_count)
        else:
            own_batch = own_rows // slot_count
            is_live = own_rows % slot_count < jnp.take(lengths, own_batch)
            own_slot = jnp.clip(jnp.take(starts, own_batch) + own_rows % slot_count, 0, live_count - 1)
            own_values = jnp.take(all_values, own_slot)
        ref_logprob = jnp.where(is_live, own_values, 0.0)
        ratio_log = jnp.clip(ref_logprob - policy_logprobs, -20.0, 20.0)
        kl_value = jnp.where(is_live, jnp.minimum(jnp.exp(ratio_log) - ratio_log - 1.0, 10.0), 0.0)
        return (ref_logprob, kl_value)

    return on_device


def solution(mesh):
    return jax.shard_map(
        make_body(dp_ring(mesh)),
        mesh=mesh,
        in_specs=(P("dp", "vocab"), P("vocab", "dp"), P(), P(), P("dp")),
        out_specs=(P("dp"), P("dp")),
        check_vma=False,
    )
```

```python
import numpy as np
import jax
import jax.numpy as jnp
from jax import lax
from jax.sharding import PartitionSpec as P

MB = 8


def dp_ring(mesh):
    size = mesh.shape["dp"]
    try:
        coords = [tuple(dev.coords) for dev in mesh.devices[:, 0]]
        xs = sorted({c[0] for c in coords})
        zs = sorted({c[2] for c in coords})
        if len(xs) * len(zs) != size or len(zs) % 2:
            raise ValueError
        where = {(c[0], c[2]): i for i, c in enumerate(coords)}
        order = [where[(xs[0], z)] for z in zs]
        for row, z in enumerate(reversed(zs)):
            cols = xs[1:] if row % 2 == 0 else list(reversed(xs[1:]))
            order += [where[(x, z)] for x in cols]
        if sorted(order) != list(range(size)):
            raise ValueError
        return order
    except Exception:
        return list(range(size))


def ring_gather(block, ring, rows, weight):
    size = len(ring)
    pos_of = np.argsort(np.asarray(ring))
    fwd = [(ring[i], ring[(i + 1) % size]) for i in range(size)]
    bwd = [(ring[(i + 1) % size], ring[i]) for i in range(size)]
    slots = [None] * size
    slots[0] = block
    ahead, behind = block, block
    count = block.shape[0]
    for step in range(1, size // 2 + 1):
        if step == size - step and count % 32 == 0:
            front = lax.ppermute(ahead[:count // 2], "dp", fwd)
            back = lax.ppermute(behind[count // 2:], "dp", bwd)
            slots[step] = jnp.concatenate([front, back])
            continue
        ahead = lax.ppermute(ahead, "dp", fwd)
        slots[step] = ahead
        if step < size - step:
            behind = lax.ppermute(behind, "dp", bwd)
            slots[size - step] = behind
    count = block.shape[0]
    me = jnp.sum(jnp.where(jnp.arange(size) == lax.axis_index("dp"), jnp.asarray(pos_of, jnp.int32), 0))
    slot_of = (me - jnp.asarray(pos_of, jnp.int32)) % size
    owner = rows // count
    hit = owner[None, :] == jnp.arange(size, dtype=jnp.int32)[:, None]
    where = jnp.sum(jnp.where(hit, slot_of[:, None], 0), axis=0) * count + rows % count
    products = [jnp.dot(part, weight, preferred_element_type=jnp.float32) for part in slots]
    return jnp.take(jnp.concatenate(products), where, axis=0)


def halving_scatter(partial, size):
    me = lax.axis_index("vocab")
    first = jnp.int32(0)
    bit = 1
    while bit < size:
        half = partial.shape[0] // 2
        pairs = partial.reshape(2, half, partial.shape[1])
        side = (me // bit) % 2
        keep = jnp.take(pairs, side, axis=0)
        send = jnp.take(pairs, 1 - side, axis=0)
        got = lax.ppermute(send, "vocab", [(i, i ^ bit) for i in range(size)])
        partial = keep + got
        first = first + side * half
        bit *= 2
    return partial, first


def merge_pair(stats, other):
    top = jnp.maximum(stats[0], other[0])
    total = stats[1] * jnp.exp(stats[0] - top) + other[1] * jnp.exp(other[0] - top)
    return jnp.stack([top, total, stats[2] + other[2]])


def merge_stats(stats, size):
    bit = 1
    while bit < size:
        if bit * 4 <= size:
            got = [lax.ppermute(stats, "dp", [(i, i ^ (bit * k)) for i in range(size)]) for k in (1, 2, 3)]
            stats = merge_pair(merge_pair(stats, got[0]), merge_pair(got[1], got[2]))
            bit *= 4
        else:
            stats = merge_pair(stats, lax.ppermute(stats, "dp", [(i, i ^ bit) for i in range(size)]))
            bit *= 2
    return stats


def doubling_gather(values, first, size):
    me = lax.axis_index("vocab")
    total = values.shape[0] * size
    out = jnp.zeros((total,), values.dtype)
    out = lax.dynamic_update_slice(out, values, (first,))
    bit = 1
    while bit < size:
        other = lax.ppermute(out, "vocab", [(i, i ^ bit) for i in range(size)])
        out = out + other
        bit *= 2
    return out


def make_body(ring):
    def on_device(hidden, head_weight, lengths, targets, policy_logprobs):
        row_count = hidden.shape[0]
        dp_size = lax.axis_size("dp")
        vocab_size = lax.axis_size("vocab")
        all_rows = row_count * dp_size
        slot_count = all_rows // MB
        tile_width = head_weight.shape[1]
        col_start = lax.axis_index("dp") * tile_width
        live_count = all_rows * 5 // 8
        ends = jnp.sum(jnp.where(jnp.arange(MB)[None, :] <= jnp.arange(MB)[:, None], lengths[None, :], 0), axis=1)
        starts = ends - lengths
        packed = jnp.arange(live_count, dtype=jnp.int32)
        batch_hit = ends[:, None] <= packed[None, :]
        batch_of = jnp.sum(batch_hit.astype(jnp.int32), axis=0)
        in_batch = packed - jnp.sum(jnp.where(batch_of[None, :] == jnp.arange(MB, dtype=jnp.int32)[:, None], starts[:, None], 0), axis=0)
        live_rows = batch_of * slot_count + in_batch
        partial = ring_gather(hidden, ring, live_rows, head_weight)
        logits, first = halving_scatter(partial, vocab_size)
        share = logits.shape[0]
        row_targets = jnp.take(targets, lax.dynamic_slice_in_dim(live_rows, first, share))
        highest = jnp.max(logits, axis=1)
        exp_total = jnp.sum(jnp.exp(logits - highest[:, None]), axis=1)
        columns = col_start + lax.broadcasted_iota(jnp.int32, logits.shape, 1)
        picked = jnp.sum(jnp.where(columns == row_targets[:, None], logits, 0.0), axis=1)
        stats = merge_stats(jnp.stack([highest, exp_total, picked]), dp_size)
        logprob = stats[2] - (stats[0] + jnp.log(stats[1]))
        all_values = doubling_gather(logprob, first, vocab_size)
        own_rows = lax.axis_index("dp") * row_count + jnp.arange(row_count, dtype=jnp.int32)
        if slot_count % row_count == 0:
            own_batch = lax.axis_index("dp") * row_count // slot_count
            hit = jnp.arange(MB) == own_batch
            own_length = jnp.sum(jnp.where(hit, lengths, 0))
            own_start = jnp.sum(jnp.where(hit, starts, 0))
            offset = lax.axis_index("dp") * row_count % slot_count
            is_live = offset + jnp.arange(row_count, dtype=jnp.int32) < own_length
            padded = jnp.concatenate([all_values, jnp.zeros((row_count,), all_values.dtype)])
            own_values = lax.dynamic_slice_in_dim(padded, jnp.clip(own_start + offset, 0, live_count), row_count)
        else:
            own_batch = own_rows // slot_count
            is_live = own_rows % slot_count < jnp.take(lengths, own_batch)
            own_slot = jnp.clip(jnp.take(starts, own_batch) + own_rows % slot_count, 0, live_count - 1)
            own_values = jnp.take(all_values, own_slot)
        ref_logprob = jnp.where(is_live, own_values, 0.0)
        ratio_log = jnp.clip(ref_logprob - policy_logprobs, -20.0, 20.0)
        kl_value = jnp.where(is_live, jnp.minimum(jnp.exp(ratio_log) - ratio_log - 1.0, 10.0), 0.0)
        return (ref_logprob, kl_value)

    return on_device


def solution(mesh):
    return jax.shard_map(
        make_body(dp_ring(mesh)),
        mesh=mesh,
        in_specs=(P("dp", "vocab"), P("vocab", "dp"), P(), P(), P("dp")),
        out_specs=(P("dp"), P("dp")),
        check_vma=False,
    )
```

```python
import numpy as np
import jax
import jax.numpy as jnp
from jax import lax
from jax.sharding import PartitionSpec as P

MB = 8


def dp_ring(mesh):
    size = mesh.shape["dp"]
    try:
        coords = [tuple(dev.coords) for dev in mesh.devices[:, 0]]
        xs = sorted({c[0] for c in coords})
        zs = sorted({c[2] for c in coords})
        if len(xs) * len(zs) != size or len(zs) % 2:
            raise ValueError
        where = {(c[0], c[2]): i for i, c in enumerate(coords)}
        order = [where[(xs[0], z)] for z in zs]
        for row, z in enumerate(reversed(zs)):
            cols = xs[1:] if row % 2 == 0 else list(reversed(xs[1:]))
            order += [where[(x, z)] for x in cols]
        if sorted(order) != list(range(size)):
            raise ValueError
        return order
    except Exception:
        return list(range(size))


def ring_gather(block, ring, rows):
    size = len(ring)
    pos_of = np.argsort(np.asarray(ring))
    fwd = [(ring[i], ring[(i + 1) % size]) for i in range(size)]
    bwd = [(ring[(i + 1) % size], ring[i]) for i in range(size)]
    count = block.shape[0]
    lanes = 2 if count % 32 == 0 else 1
    parts = [block[i * count // lanes:(i + 1) * count // lanes] for i in range(lanes)]
    slots = [None] * size
    slots[0] = block
    ahead, behind = list(parts), list(parts)
    for step in range(1, size // 2 + 1):
        ahead = [lax.ppermute(piece, "dp", fwd) for piece in ahead]
        slots[step] = jnp.concatenate(ahead) if lanes > 1 else ahead[0]
        if step < size - step:
            behind = [lax.ppermute(piece, "dp", bwd) for piece in behind]
            slots[size - step] = jnp.concatenate(behind) if lanes > 1 else behind[0]
    count = block.shape[0]
    stacked = jnp.stack(slots).reshape(-1, block.shape[1])
    me = jnp.asarray(pos_of, jnp.int32)[lax.axis_index("dp")]
    slot_of = (me - jnp.asarray(pos_of, jnp.int32)) % size
    owner = rows // count
    hit = owner[None, :] == jnp.arange(size, dtype=jnp.int32)[:, None]
    where = jnp.sum(jnp.where(hit, slot_of[:, None], 0), axis=0) * count + rows % count
    choose = lax.broadcasted_iota(jnp.int32, (stacked.shape[0], where.shape[0]), 0) == where[None, :]
    picked = lax.dot_general(choose.astype(stacked.dtype), stacked, (((0,), (0,)), ((), ())), preferred_element_type=jnp.float32)
    return lax.optimization_barrier(picked.astype(stacked.dtype))


def halving_scatter(partial, size):
    me = lax.axis_index("vocab")
    first = jnp.int32(0)
    bit = 1
    while bit < size:
        half = partial.shape[0] // 2
        pairs = partial.reshape(2, half, partial.shape[1])
        side = (me // bit) % 2
        keep = jnp.take(pairs, side, axis=0)
        send = jnp.take(pairs, 1 - side, axis=0)
        got = lax.ppermute(send, "vocab", [(i, i ^ bit) for i in range(size)])
        partial = keep + got
        first = first + side * half
        bit *= 2
    return partial, first


def merge_pair(stats, other):
    top = jnp.maximum(stats[0], other[0])
    total = stats[1] * jnp.exp(stats[0] - top) + other[1] * jnp.exp(other[0] - top)
    return jnp.stack([top, total, stats[2] + other[2]])


def merge_stats(stats, size):
    bit = 1
    while bit < size:
        if bit * 4 <= size:
            got = [lax.ppermute(stats, "dp", [(i, i ^ (bit * k)) for i in range(size)]) for k in (1, 2, 3)]
            stats = merge_pair(merge_pair(stats, got[0]), merge_pair(got[1], got[2]))
            bit *= 4
        else:
            stats = merge_pair(stats, lax.ppermute(stats, "dp", [(i, i ^ bit) for i in range(size)]))
            bit *= 2
    return stats


def doubling_gather(values, first, size):
    me = lax.axis_index("vocab")
    total = values.shape[0] * size
    out = jnp.zeros((total,), values.dtype)
    out = lax.dynamic_update_slice(out, values, (first,))
    bit = 1
    while bit < size:
        other = lax.ppermute(out, "vocab", [(i, i ^ bit) for i in range(size)])
        out = out + other
        bit *= 2
    return out


def make_body(ring):
    def on_device(hidden, head_weight, lengths, targets, policy_logprobs):
        row_count = hidden.shape[0]
        dp_size = lax.axis_size("dp")
        vocab_size = lax.axis_size("vocab")
        all_rows = row_count * dp_size
        slot_count = all_rows // MB
        tile_width = head_weight.shape[1]
        col_start = lax.axis_index("dp") * tile_width
        live_count = all_rows * 5 // 8
        ends = jnp.cumsum(lengths)
        starts = ends - lengths
        packed = jnp.arange(live_count, dtype=jnp.int32)
        batch_hit = ends[:, None] <= packed[None, :]
        batch_of = jnp.sum(batch_hit.astype(jnp.int32), axis=0)
        in_batch = packed - jnp.sum(jnp.where(batch_of[None, :] == jnp.arange(MB, dtype=jnp.int32)[:, None], starts[:, None], 0), axis=0)
        live_rows = batch_of * slot_count + in_batch
        full_rows = ring_gather(hidden, ring, live_rows)
        partial = jnp.dot(full_rows, head_weight, preferred_element_type=jnp.float32)
        logits, first = halving_scatter(partial, vocab_size)
        share = logits.shape[0]
        row_targets = jnp.take(targets, lax.dynamic_slice_in_dim(live_rows, first, share))
        highest = jnp.max(logits, axis=1)
        exp_total = jnp.sum(jnp.exp(logits - highest[:, None]), axis=1)
        columns = col_start + lax.broadcasted_iota(jnp.int32, logits.shape, 1)
        picked = jnp.sum(jnp.where(columns == row_targets[:, None], logits, 0.0), axis=1)
        stats = merge_stats(jnp.stack([highest, exp_total, picked]), dp_size)
        logprob = stats[2] - (stats[0] + jnp.log(stats[1]))
        all_values = doubling_gather(logprob, first, vocab_size)
        own_rows = lax.axis_index("dp") * row_count + jnp.arange(row_count, dtype=jnp.int32)
        own_batch = own_rows // slot_count
        is_live = own_rows % slot_count < jnp.take(lengths, own_batch)
        own_slot = jnp.clip(jnp.take(starts, own_batch) + own_rows % slot_count, 0, live_count - 1)
        own_values = jnp.take(all_values, own_slot)
        ref_logprob = jnp.where(is_live, own_values, 0.0)
        ratio_log = jnp.clip(ref_logprob - policy_logprobs, -20.0, 20.0)
        kl_value = jnp.where(is_live, jnp.minimum(jnp.exp(ratio_log) - ratio_log - 1.0, 10.0), 0.0)
        return (ref_logprob, kl_value)

    return on_device


def solution(mesh):
    return jax.shard_map(
        make_body(dp_ring(mesh)),
        mesh=mesh,
        in_specs=(P("dp", "vocab"), P("vocab", "dp"), P(), P(), P("dp")),
        out_specs=(P("dp"), P("dp")),
        check_vma=False,
    )
```

```python
import numpy as np
import jax
import jax.numpy as jnp
from jax import lax
from jax.sharding import PartitionSpec as P
from jax.experimental import pallas as pl
from jax.experimental.pallas import tpu as pltpu

MB = 8


def dp_ring(mesh):
    size = mesh.shape["dp"]
    try:
        coords = [tuple(dev.coords) for dev in mesh.devices[:, 0]]
        xs = sorted({c[0] for c in coords})
        zs = sorted({c[2] for c in coords})
        if len(xs) * len(zs) != size or len(zs) % 2:
            raise ValueError
        where = {(c[0], c[2]): i for i, c in enumerate(coords)}
        order = [where[(xs[0], z)] for z in zs]
        for row, z in enumerate(reversed(zs)):
            cols = xs[1:] if row % 2 == 0 else list(reversed(xs[1:]))
            order += [where[(x, z)] for x in cols]
        if sorted(order) != list(range(size)):
            raise ValueError
        return order
    except Exception:
        return list(range(size))


def ring_gather(block, ring, rows):
    size = len(ring)
    pos_of = np.argsort(np.asarray(ring))
    fwd = [(ring[i], ring[(i + 1) % size]) for i in range(size)]
    bwd = [(ring[(i + 1) % size], ring[i]) for i in range(size)]
    slots = [None] * size
    slots[0] = block
    ahead, behind = block, block
    for step in range(1, size // 2 + 1):
        ahead = lax.ppermute(ahead, "dp", fwd)
        slots[step] = ahead
        if step < size - step:
            behind = lax.ppermute(behind, "dp", bwd)
            slots[size - step] = behind
    count = block.shape[0]
    stacked = jnp.stack(slots).reshape(-1, block.shape[1])
    me = jnp.asarray(pos_of, jnp.int32)[lax.axis_index("dp")]
    slot_of = (me - jnp.asarray(pos_of, jnp.int32)) % size
    owner = rows // count
    hit = owner[None, :] == jnp.arange(size, dtype=jnp.int32)[:, None]
    where = jnp.sum(jnp.where(hit, slot_of[:, None], 0), axis=0) * count + rows % count
    choose = lax.broadcasted_iota(jnp.int32, (stacked.shape[0], where.shape[0]), 0) == where[None, :]
    picked = lax.dot_general(choose.astype(stacked.dtype), stacked, (((0,), (0,)), ((), ())), preferred_element_type=jnp.float32)
    return lax.optimization_barrier(picked.astype(stacked.dtype))


def product_kernel(rows_ref, weight_ref, out_ref):
    out_ref[...] = jnp.dot(rows_ref[...], weight_ref[...], preferred_element_type=jnp.float32)


def column_product(rows, weight, first, width, tile):
    count, depth = rows.shape
    base = first // tile
    return pl.pallas_call(
        product_kernel,
        out_shape=jax.ShapeDtypeStruct((count, width), jnp.float32),
        grid=(width // tile,),
        in_specs=[pl.BlockSpec((count, depth), lambda j: (0, 0)), pl.BlockSpec((depth, tile), lambda j: (0, base + j))],
        out_specs=pl.BlockSpec((count, tile), lambda j: (0, j)),
    )(rows, weight)


def halving_scatter(partial, size):
    me = lax.axis_index("vocab")
    first = jnp.int32(0)
    bit = 1
    while bit < size:
        half = partial.shape[0] // 2
        pairs = partial.reshape(2, half, partial.shape[1])
        side = (me // bit) % 2
        keep = jnp.take(pairs, side, axis=0)
        send = jnp.take(pairs, 1 - side, axis=0)
        got = lax.ppermute(send, "vocab", [(i, i ^ bit) for i in range(size)])
        partial = keep + got
        first = first + side * half
        bit *= 2
    return partial, first


def merge_pair(stats, other):
    top = jnp.maximum(stats[0], other[0])
    total = stats[1] * jnp.exp(stats[0] - top) + other[1] * jnp.exp(other[0] - top)
    return jnp.stack([top, total, stats[2] + other[2]])


def merge_stats(stats, size):
    bit = 1
    while bit < size:
        if bit * 4 <= size:
            got = [lax.ppermute(stats, "dp", [(i, i ^ (bit * k)) for i in range(size)]) for k in (1, 2, 3)]
            stats = merge_pair(merge_pair(stats, got[0]), merge_pair(got[1], got[2]))
            bit *= 4
        else:
            stats = merge_pair(stats, lax.ppermute(stats, "dp", [(i, i ^ bit) for i in range(size)]))
            bit *= 2
    return stats


def doubling_gather(values, first, size):
    me = lax.axis_index("vocab")
    total = values.shape[0] * size
    out = jnp.zeros((total,), values.dtype)
    out = lax.dynamic_update_slice(out, values, (first,))
    bit = 1
    while bit < size:
        other = lax.ppermute(out, "vocab", [(i, i ^ bit) for i in range(size)])
        out = out + other
        bit *= 2
    return out


def make_body(ring):
    def on_device(hidden, head_weight, lengths, targets, policy_logprobs):
        row_count = hidden.shape[0]
        dp_size = lax.axis_size("dp")
        vocab_size = lax.axis_size("vocab")
        all_rows = row_count * dp_size
        slot_count = all_rows // MB
        tile_width = head_weight.shape[1]
        col_start = lax.axis_index("dp") * tile_width
        live_count = all_rows * 5 // 8
        ends = jnp.cumsum(lengths)
        starts = ends - lengths
        packed = jnp.arange(live_count, dtype=jnp.int32)
        batch_hit = ends[:, None] <= packed[None, :]
        batch_of = jnp.sum(batch_hit.astype(jnp.int32), axis=0)
        in_batch = packed - jnp.sum(jnp.where(batch_of[None, :] == jnp.arange(MB, dtype=jnp.int32)[:, None], starts[:, None], 0), axis=0)
        live_rows = batch_of * slot_count + in_batch
        full_rows = ring_gather(hidden, ring, live_rows)
        pieces = 2 if tile_width % 1024 == 0 else 1
        width = tile_width // pieces
        parts = []
        for piece in range(pieces):
            partial = column_product(full_rows, head_weight, piece * width, width, 512 if width % 512 == 0 else width)
            logits, first = halving_scatter(partial, vocab_size)
            share = logits.shape[0]
            row_targets = jnp.take(targets, lax.dynamic_slice_in_dim(live_rows, first, share))
            highest = jnp.max(logits, axis=1)
            exp_total = jnp.sum(jnp.exp(logits - highest[:, None]), axis=1)
            columns = col_start + piece * width + lax.broadcasted_iota(jnp.int32, logits.shape, 1)
            picked = jnp.sum(jnp.where(columns == row_targets[:, None], logits, 0.0), axis=1)
            parts.append((highest, exp_total, picked))
        highest = parts[0][0]
        for part in parts[1:]:
            highest = jnp.maximum(highest, part[0])
        exp_total = sum(part[1] * jnp.exp(part[0] - highest) for part in parts)
        picked = sum(part[2] for part in parts)
        stats = merge_stats(jnp.stack([highest, exp_total, picked]), dp_size)
        logprob = stats[2] - (stats[0] + jnp.log(stats[1]))
        all_values = doubling_gather(logprob, first, vocab_size)
        own_rows = lax.axis_index("dp") * row_count + jnp.arange(row_count, dtype=jnp.int32)
        own_batch = own_rows // slot_count
        is_live = own_rows % slot_count < jnp.take(lengths, own_batch)
        own_slot = jnp.clip(jnp.take(starts, own_batch) + own_rows % slot_count, 0, live_count - 1)
        own_values = jnp.take(all_values, own_slot)
        ref_logprob = jnp.where(is_live, own_values, 0.0)
        ratio_log = jnp.clip(ref_logprob - policy_logprobs, -20.0, 20.0)
        kl_value = jnp.where(is_live, jnp.minimum(jnp.exp(ratio_log) - ratio_log - 1.0, 10.0), 0.0)
        return (ref_logprob, kl_value)

    return on_device


def solution(mesh):
    return jax.shard_map(
        make_body(dp_ring(mesh)),
        mesh=mesh,
        in_specs=(P("dp", "vocab"), P("vocab", "dp"), P(), P(), P("dp")),
        out_specs=(P("dp"), P("dp")),
        check_vma=False,
    )
```

```python
import numpy as np
import jax
import jax.numpy as jnp
from jax import lax
from jax.sharding import PartitionSpec as P

MB = 8


def dp_ring(mesh):
    size = mesh.shape["dp"]
    try:
        coords = [tuple(dev.coords) for dev in mesh.devices[:, 0]]
        xs = sorted({c[0] for c in coords})
        zs = sorted({c[2] for c in coords})
        if len(xs) * len(zs) != size or len(zs) % 2:
            raise ValueError
        where = {(c[0], c[2]): i for i, c in enumerate(coords)}
        order = [where[(xs[0], z)] for z in zs]
        for row, z in enumerate(reversed(zs)):
            cols = xs[1:] if row % 2 == 0 else list(reversed(xs[1:]))
            order += [where[(x, z)] for x in cols]
        if sorted(order) != list(range(size)):
            raise ValueError
        return order
    except Exception:
        return list(range(size))


def ring_gather(block, ring, rows):
    size = len(ring)
    pos_of = np.argsort(np.asarray(ring))
    fwd = [(ring[i], ring[(i + 1) % size]) for i in range(size)]
    bwd = [(ring[(i + 1) % size], ring[i]) for i in range(size)]
    slots = [None] * size
    slots[0] = block
    ahead, behind = block, block
    for step in range(1, size // 2 + 1):
        ahead = lax.ppermute(ahead, "dp", fwd)
        slots[step] = ahead
        if step < size - step:
            behind = lax.ppermute(behind, "dp", bwd)
            slots[size - step] = behind
    count = block.shape[0]
    stacked = jnp.stack(slots).reshape(-1, block.shape[1])
    me = jnp.asarray(pos_of, jnp.int32)[lax.axis_index("dp")]
    slot_of = (me - jnp.asarray(pos_of, jnp.int32)) % size
    owner = rows // count
    hit = owner[None, :] == jnp.arange(size, dtype=jnp.int32)[:, None]
    where = jnp.sum(jnp.where(hit, slot_of[:, None], 0), axis=0) * count + rows % count
    where = jnp.where(rows < 0, -1, where)
    choose = lax.broadcasted_iota(jnp.int32, (stacked.shape[0], where.shape[0]), 0) == where[None, :]
    picked = lax.dot_general(choose.astype(stacked.dtype), stacked, (((0,), (0,)), ((), ())), preferred_element_type=jnp.float32)
    return picked.astype(stacked.dtype)


def halving_scatter(partial, size):
    bit = 1
    while bit < size:
        half = partial.shape[0] // 2
        got = lax.ppermute(partial[:half], "vocab", [(i, i ^ bit) for i in range(size)])
        partial = partial[half:] + got
        bit *= 2
    return partial


def send_first_order(count, size):
    me = lax.axis_index("vocab")
    place = jnp.arange(count, dtype=jnp.int32)
    canon = jnp.zeros((count,), jnp.int32)
    first = jnp.int32(0)
    span, bit, level = count, 1, 0
    while bit < size:
        span //= 2
        side = (me // bit) % 2
        digit = (place // span) % 2
        canon = canon + ((1 - side) ^ digit) * span
        first = first + side * span
        bit *= 2
        level += 1
    return canon + place % span, first


def merge_stats(stats, size):
    bit = 1
    while bit < size:
        other = lax.ppermute(stats, "dp", [(i, i ^ bit) for i in range(size)])
        top = jnp.maximum(stats[0], other[0])
        total = stats[1] * jnp.exp(stats[0] - top) + other[1] * jnp.exp(other[0] - top)
        stats = jnp.stack([top, total, stats[2] + other[2]])
        bit *= 2
    return stats


def doubling_gather(values, first, size):
    me = lax.axis_index("vocab")
    total = values.shape[0] * size
    out = jnp.zeros((total,), values.dtype)
    out = lax.dynamic_update_slice(out, values, (first,))
    bit = 1
    while bit < size:
        other = lax.ppermute(out, "vocab", [(i, i ^ bit) for i in range(size)])
        out = out + other
        bit *= 2
    return out


def make_body(ring):
    def on_device(hidden, head_weight, lengths, targets, policy_logprobs):
        row_count = hidden.shape[0]
        dp_size = lax.axis_size("dp")
        vocab_size = lax.axis_size("vocab")
        all_rows = row_count * dp_size
        slot_count = all_rows // MB
        tile_width = head_weight.shape[1]
        col_start = lax.axis_index("dp") * tile_width
        live_count = all_rows * 5 // 8
        ends = jnp.cumsum(lengths)
        starts = ends - lengths
        packed, first = send_first_order(live_count, vocab_size)
        batch_hit = ends[:, None] <= packed[None, :]
        batch_of = jnp.sum(batch_hit.astype(jnp.int32), axis=0)
        in_batch = packed - jnp.sum(jnp.where(batch_of[None, :] == jnp.arange(MB, dtype=jnp.int32)[:, None], starts[:, None], 0), axis=0)
        live_rows = batch_of * slot_count + in_batch
        is_own = (live_rows >= lax.axis_index("dp") * row_count) & (live_rows < lax.axis_index("dp") * row_count + row_count)
        full_rows = ring_gather(hidden, ring, jnp.where(is_own, -1, live_rows))
        share = live_count // vocab_size
        row_targets = lax.dynamic_slice_in_dim(live_rows, live_count - share, share)
        row_targets = jnp.take(targets, row_targets)
        own_first = lax.axis_index("dp") * row_count
        own_partial = jnp.dot(hidden, head_weight, preferred_element_type=jnp.float32)
        own_pick = (live_rows - own_first)[:, None] == lax.broadcasted_iota(jnp.int32, (live_count, row_count), 1)
        own_spread = jnp.dot(own_pick.astype(jnp.float32), own_partial, precision=lax.Precision.HIGHEST, preferred_element_type=jnp.float32)
        pieces = 2 if tile_width % 256 == 0 else 1
        width = tile_width // pieces
        parts = []
        for piece in range(pieces):
            partial = jnp.dot(full_rows, head_weight[:, piece * width:(piece + 1) * width], preferred_element_type=jnp.float32)
            logits = halving_scatter(partial + own_spread[:, piece * width:(piece + 1) * width], vocab_size)
            highest = jnp.max(logits, axis=1)
            exp_total = jnp.sum(jnp.exp(logits - highest[:, None]), axis=1)
            columns = col_start + piece * width + lax.broadcasted_iota(jnp.int32, logits.shape, 1)
            picked = jnp.sum(jnp.where(columns == row_targets[:, None], logits, 0.0), axis=1)
            parts.append((highest, exp_total, picked))
        highest = parts[0][0]
        for part in parts[1:]:
            highest = jnp.maximum(highest, part[0])
        exp_total = sum(part[1] * jnp.exp(part[0] - highest) for part in parts)
        picked = sum(part[2] for part in parts)
        stats = merge_stats(jnp.stack([highest, exp_total, picked]), dp_size)
        logprob = stats[2] - (stats[0] + jnp.log(stats[1]))
        all_values = doubling_gather(logprob, first, vocab_size)
        own_rows = lax.axis_index("dp") * row_count + jnp.arange(row_count, dtype=jnp.int32)
        own_batch = own_rows // slot_count
        is_live = own_rows % slot_count < jnp.take(lengths, own_batch)
        own_slot = jnp.clip(jnp.take(starts, own_batch) + own_rows % slot_count, 0, live_count - 1)
        own_values = jnp.take(all_values, own_slot)
        ref_logprob = jnp.where(is_live, own_values, 0.0)
        ratio_log = jnp.clip(ref_logprob - policy_logprobs, -20.0, 20.0)
        kl_value = jnp.where(is_live, jnp.minimum(jnp.exp(ratio_log) - ratio_log - 1.0, 10.0), 0.0)
        return (ref_logprob, kl_value)

    return on_device


def solution(mesh):
    return jax.shard_map(
        make_body(dp_ring(mesh)),
        mesh=mesh,
        in_specs=(P("dp", "vocab"), P("vocab", "dp"), P(), P(), P("dp")),
        out_specs=(P("dp"), P("dp")),
        check_vma=False,
    )
```

```python
import numpy as np
import jax
import jax.numpy as jnp
from jax import lax
from jax.sharding import PartitionSpec as P

MB = 8


def dp_ring(mesh):
    size = mesh.shape["dp"]
    try:
        coords = [tuple(dev.coords) for dev in mesh.devices[:, 0]]
        xs = sorted({c[0] for c in coords})
        zs = sorted({c[2] for c in coords})
        if len(xs) * len(zs) != size or len(zs) % 2:
            raise ValueError
        where = {(c[0], c[2]): i for i, c in enumerate(coords)}
        order = [where[(xs[0], z)] for z in zs]
        for row, z in enumerate(reversed(zs)):
            cols = xs[1:] if row % 2 == 0 else list(reversed(xs[1:]))
            order += [where[(x, z)] for x in cols]
        if sorted(order) != list(range(size)):
            raise ValueError
        return order
    except Exception:
        return list(range(size))


def ring_gather(block, ring, rows):
    size = len(ring)
    pos_of = np.argsort(np.asarray(ring))
    fwd = [(ring[i], ring[(i + 1) % size]) for i in range(size)]
    bwd = [(ring[(i + 1) % size], ring[i]) for i in range(size)]
    slots = [None] * size
    slots[0] = block
    ahead, behind = block, block
    for step in range(1, size // 2 + 1):
        ahead = lax.ppermute(ahead, "dp", fwd)
        slots[step] = ahead
        if step < size - step:
            behind = lax.ppermute(behind, "dp", bwd)
            slots[size - step] = behind
    count = block.shape[0]
    stacked = jnp.stack(slots).reshape(-1, block.shape[1])
    me = jnp.asarray(pos_of, jnp.int32)[lax.axis_index("dp")]
    slot_of = (me - jnp.asarray(pos_of, jnp.int32)) % size
    owner = rows // count
    hit = owner[None, :] == jnp.arange(size, dtype=jnp.int32)[:, None]
    where = jnp.sum(jnp.where(hit, slot_of[:, None], 0), axis=0) * count + rows % count
    choose = lax.broadcasted_iota(jnp.int32, (stacked.shape[0], where.shape[0]), 0) == where[None, :]
    picked = lax.dot_general(choose.astype(stacked.dtype), stacked, (((0,), (0,)), ((), ())), preferred_element_type=jnp.float32)
    return lax.optimization_barrier(picked.astype(stacked.dtype))


def halving_scatter(partial, size):
    me = lax.axis_index("vocab")
    first = jnp.int32(0)
    bit = 1
    while bit < size:
        half = partial.shape[0] // 2
        pairs = partial.reshape(2, half, partial.shape[1])
        side = (me // bit) % 2
        keep = jnp.take(pairs, side, axis=0)
        send = jnp.take(pairs, 1 - side, axis=0)
        got = lax.ppermute(send, "vocab", [(i, i ^ bit) for i in range(size)])
        partial = keep + got
        first = first + side * half
        bit *= 2
    return partial, first


def merge_pair(stats, other):
    top = jnp.maximum(stats[0], other[0])
    total = stats[1] * jnp.exp(stats[0] - top) + other[1] * jnp.exp(other[0] - top)
    return jnp.stack([top, total, stats[2] + other[2]])


def merge_stats(stats, size):
    bits = []
    bit = 1
    while bit < size:
        bits.append(bit)
        bit *= 2
    while bits:
        if len(bits) >= 2:
            low, high = bits[-2], bits[-1]
            bits = bits[:-2]
            got = [lax.ppermute(stats, "dp", [(i, i ^ flip) for i in range(size)]) for flip in (low, high, low | high)]
            stats = merge_pair(merge_pair(stats, got[0]), merge_pair(got[1], got[2]))
        else:
            stats = merge_pair(stats, lax.ppermute(stats, "dp", [(i, i ^ bits[0]) for i in range(size)]))
            bits = []
    return stats


def doubling_gather(values, first, size):
    me = lax.axis_index("vocab")
    total = values.shape[0] * size
    out = jnp.zeros((total,), values.dtype)
    out = lax.dynamic_update_slice(out, values, (first,))
    bit = 1
    while bit < size:
        other = lax.ppermute(out, "vocab", [(i, i ^ bit) for i in range(size)])
        out = out + other
        bit *= 2
    return out


def make_body(ring):
    def on_device(hidden, head_weight, lengths, targets, policy_logprobs):
        row_count = hidden.shape[0]
        dp_size = lax.axis_size("dp")
        vocab_size = lax.axis_size("vocab")
        all_rows = row_count * dp_size
        slot_count = all_rows // MB
        tile_width = head_weight.shape[1]
        col_start = lax.axis_index("dp") * tile_width
        live_count = all_rows * 5 // 8
        ends = jnp.cumsum(lengths)
        starts = ends - lengths
        packed = jnp.arange(live_count, dtype=jnp.int32)
        batch_hit = ends[:, None] <= packed[None, :]
        batch_of = jnp.sum(batch_hit.astype(jnp.int32), axis=0)
        in_batch = packed - jnp.sum(jnp.where(batch_of[None, :] == jnp.arange(MB, dtype=jnp.int32)[:, None], starts[:, None], 0), axis=0)
        live_rows = batch_of * slot_count + in_batch
        full_rows = ring_gather(hidden, ring, live_rows)
        partial = jnp.dot(full_rows, head_weight, preferred_element_type=jnp.float32)
        logits, first = halving_scatter(partial, vocab_size)
        share = logits.shape[0]
        row_targets = jnp.take(targets, lax.dynamic_slice_in_dim(live_rows, first, share))
        highest = jnp.max(logits, axis=1)
        exp_total = jnp.sum(jnp.exp(logits - highest[:, None]), axis=1)
        columns = col_start + lax.broadcasted_iota(jnp.int32, logits.shape, 1)
        picked = jnp.sum(jnp.where(columns == row_targets[:, None], logits, 0.0), axis=1)
        stats = merge_stats(jnp.stack([highest, exp_total, picked]), dp_size)
        logprob = stats[2] - (stats[0] + jnp.log(stats[1]))
        all_values = doubling_gather(logprob, first, vocab_size)
        own_rows = lax.axis_index("dp") * row_count + jnp.arange(row_count, dtype=jnp.int32)
        own_batch = own_rows // slot_count
        is_live = own_rows % slot_count < jnp.take(lengths, own_batch)
        own_slot = jnp.clip(jnp.take(starts, own_batch) + own_rows % slot_count, 0, live_count - 1)
        own_values = jnp.take(all_values, own_slot)
        ref_logprob = jnp.where(is_live, own_values, 0.0)
        ratio_log = jnp.clip(ref_logprob - policy_logprobs, -20.0, 20.0)
        kl_value = jnp.where(is_live, jnp.minimum(jnp.exp(ratio_log) - ratio_log - 1.0, 10.0), 0.0)
        return (ref_logprob, kl_value)

    return on_device


def solution(mesh):
    return jax.shard_map(
        make_body(dp_ring(mesh)),
        mesh=mesh,
        in_specs=(P("dp", "vocab"), P("vocab", "dp"), P(), P(), P("dp")),
        out_specs=(P("dp"), P("dp")),
        check_vma=False,
    )
```

```python
import numpy as np
import jax
import jax.numpy as jnp
from jax import lax
from jax.sharding import PartitionSpec as P

MB = 8


def dp_ring(mesh):
    size = mesh.shape["dp"]
    try:
        coords = [tuple(dev.coords) for dev in mesh.devices[:, 0]]
        xs = sorted({c[0] for c in coords})
        zs = sorted({c[2] for c in coords})
        if len(xs) * len(zs) != size or len(zs) % 2:
            raise ValueError
        where = {(c[0], c[2]): i for i, c in enumerate(coords)}
        order = [where[(xs[0], z)] for z in zs]
        for row, z in enumerate(reversed(zs)):
            cols = xs[1:] if row % 2 == 0 else list(reversed(xs[1:]))
            order += [where[(x, z)] for x in cols]
        if sorted(order) != list(range(size)):
            raise ValueError
        return order
    except Exception:
        return list(range(size))


def ring_gather(block, ring, rows):
    size = len(ring)
    pos_of = np.argsort(np.asarray(ring))
    fwd = [(ring[i], ring[(i + 1) % size]) for i in range(size)]
    bwd = [(ring[(i + 1) % size], ring[i]) for i in range(size)]
    slots = [None] * size
    slots[0] = block
    ahead, behind = block, block
    for step in range(1, size // 2 + 1):
        ahead = lax.ppermute(ahead, "dp", fwd)
        slots[step] = ahead
        if step < size - step:
            behind = lax.ppermute(behind, "dp", bwd)
            slots[size - step] = behind
    count = block.shape[0]
    stacked = jnp.stack(slots).reshape(-1, block.shape[1])
    me = jnp.asarray(pos_of, jnp.int32)[lax.axis_index("dp")]
    slot_of = (me - jnp.asarray(pos_of, jnp.int32)) % size
    owner = rows // count
    hit = owner[None, :] == jnp.arange(size, dtype=jnp.int32)[:, None]
    where = jnp.sum(jnp.where(hit, slot_of[:, None], 0), axis=0) * count + rows % count
    choose = lax.broadcasted_iota(jnp.int32, (stacked.shape[0], where.shape[0]), 0) == where[None, :]
    picked = lax.dot_general(choose.astype(stacked.dtype), stacked, (((0,), (0,)), ((), ())), preferred_element_type=jnp.float32)
    return picked.astype(stacked.dtype)


def halving_scatter(partial, size):
    me = lax.axis_index("vocab")
    first = jnp.int32(0)
    bit = 1
    while bit < size:
        half = partial.shape[0] // 2
        pairs = partial.reshape(2, half, partial.shape[1])
        side = (me // bit) % 2
        keep = jnp.take(pairs, side, axis=0)
        send = jnp.take(pairs, 1 - side, axis=0)
        got = lax.ppermute(send, "vocab", [(i, i ^ bit) for i in range(size)])
        partial = keep + got
        first = first + side * half
        bit *= 2
    return partial, first


def merge_pair(stats, other):
    top = jnp.maximum(stats[0], other[0])
    total = stats[1] * jnp.exp(stats[0] - top) + other[1] * jnp.exp(other[0] - top)
    return jnp.stack([top, total, stats[2] + other[2]])


def merge_stats(stats, size):
    bit = 1
    while bit < size:
        if bit * 4 <= size:
            got = [lax.ppermute(stats, "dp", [(i, i ^ (bit * k)) for i in range(size)]) for k in (1, 2, 3)]
            stats = merge_pair(merge_pair(stats, got[0]), merge_pair(got[1], got[2]))
            bit *= 4
        else:
            stats = merge_pair(stats, lax.ppermute(stats, "dp", [(i, i ^ bit) for i in range(size)]))
            bit *= 2
    return stats


def doubling_gather(values, first, size):
    me = lax.axis_index("vocab")
    total = values.shape[0] * size
    out = jnp.zeros((total,), values.dtype)
    out = lax.dynamic_update_slice(out, values, (first,))
    bit = 1
    while bit < size:
        other = lax.ppermute(out, "vocab", [(i, i ^ bit) for i in range(size)])
        out = out + other
        bit *= 2
    return out


def make_body(ring):
    def on_device(hidden, head_weight, lengths, targets, policy_logprobs):
        row_count = hidden.shape[0]
        dp_size = lax.axis_size("dp")
        vocab_size = lax.axis_size("vocab")
        all_rows = row_count * dp_size
        slot_count = all_rows // MB
        tile_width = head_weight.shape[1]
        col_start = lax.axis_index("dp") * tile_width
        live_count = all_rows * 5 // 8
        ends = jnp.cumsum(lengths)
        starts = ends - lengths
        packed = jnp.arange(live_count, dtype=jnp.int32)
        batch_hit = ends[:, None] <= packed[None, :]
        batch_of = jnp.sum(batch_hit.astype(jnp.int32), axis=0)
        in_batch = packed - jnp.sum(jnp.where(batch_of[None, :] == jnp.arange(MB, dtype=jnp.int32)[:, None], starts[:, None], 0), axis=0)
        live_rows = batch_of * slot_count + in_batch
        full_rows = ring_gather(hidden, ring, live_rows)
        partial = jnp.dot(full_rows, head_weight, preferred_element_type=jnp.float32)
        logits, first = halving_scatter(partial, vocab_size)
        share = logits.shape[0]
        row_targets = jnp.take(targets, lax.dynamic_slice_in_dim(live_rows, first, share))
        highest = jnp.max(logits, axis=1)
        exp_total = jnp.sum(jnp.exp(logits - highest[:, None]), axis=1)
        columns = col_start + lax.broadcasted_iota(jnp.int32, logits.shape, 1)
        picked = jnp.sum(jnp.where(columns == row_targets[:, None], logits, 0.0), axis=1)
        stats = merge_stats(jnp.stack([highest, exp_total, picked]), dp_size)
        logprob = stats[2] - (stats[0] + jnp.log(stats[1]))
        all_values = doubling_gather(logprob, first, vocab_size)
        own_rows = lax.axis_index("dp") * row_count + jnp.arange(row_count, dtype=jnp.int32)
        own_batch = own_rows // slot_count
        is_live = own_rows % slot_count < jnp.take(lengths, own_batch)
        own_slot = jnp.clip(jnp.take(starts, own_batch) + own_rows % slot_count, 0, live_count - 1)
        own_values = jnp.take(all_values, own_slot)
        ref_logprob = jnp.where(is_live, own_values, 0.0)
        ratio_log = jnp.clip(ref_logprob - policy_logprobs, -20.0, 20.0)
        kl_value = jnp.where(is_live, jnp.minimum(jnp.exp(ratio_log) - ratio_log - 1.0, 10.0), 0.0)
        return (ref_logprob, kl_value)

    return on_device


def solution(mesh):
    return jax.shard_map(
        make_body(dp_ring(mesh)),
        mesh=mesh,
        in_specs=(P("dp", "vocab"), P("vocab", "dp"), P(), P(), P("dp")),
        out_specs=(P("dp"), P("dp")),
        check_vma=False,
    )
```

```python
import numpy as np
import jax
import jax.numpy as jnp
from jax import lax
from jax.sharding import PartitionSpec as P

MB = 8


def dp_ring(mesh):
    size = mesh.shape["dp"]
    try:
        coords = [tuple(dev.coords) for dev in mesh.devices[:, 0]]
        xs = sorted({c[0] for c in coords})
        zs = sorted({c[2] for c in coords})
        if len(xs) * len(zs) != size or len(zs) % 2:
            raise ValueError
        where = {(c[0], c[2]): i for i, c in enumerate(coords)}
        order = [where[(xs[0], z)] for z in zs]
        for row, z in enumerate(reversed(zs)):
            cols = xs[1:] if row % 2 == 0 else list(reversed(xs[1:]))
            order += [where[(x, z)] for x in cols]
        if sorted(order) != list(range(size)):
            raise ValueError
        return order
    except Exception:
        return list(range(size))


def ring_gather(block, ring, rows):
    size = len(ring)
    pos_of = np.argsort(np.asarray(ring))
    fwd = [(ring[i], ring[(i + 1) % size]) for i in range(size)]
    bwd = [(ring[(i + 1) % size], ring[i]) for i in range(size)]
    slots = [None] * size
    slots[0] = block
    ahead, behind = block, block
    for step in range(1, size // 2 + 1):
        ahead = lax.ppermute(ahead, "dp", fwd)
        slots[step] = ahead
        if step < size - step:
            behind = lax.ppermute(behind, "dp", bwd)
            slots[size - step] = behind
    count = block.shape[0]
    stacked = jnp.stack(slots).reshape(-1, block.shape[1])
    me = jnp.asarray(pos_of, jnp.int32)[lax.axis_index("dp")]
    slot_of = (me - jnp.asarray(pos_of, jnp.int32)) % size
    owner = rows // count
    hit = owner[None, :] == jnp.arange(size, dtype=jnp.int32)[:, None]
    where = jnp.sum(jnp.where(hit, slot_of[:, None], 0), axis=0) * count + rows % count
    choose = lax.broadcasted_iota(jnp.int32, (stacked.shape[0], where.shape[0]), 0) == where[None, :]
    picked = lax.dot_general(choose.astype(stacked.dtype), stacked, (((0,), (0,)), ((), ())), preferred_element_type=jnp.float32)
    return picked.astype(stacked.dtype)


def halving_scatter(partial, size):
    bit = 1
    while bit < size:
        half = partial.shape[0] // 2
        got = lax.ppermute(partial[:half], "vocab", [(i, i ^ bit) for i in range(size)])
        partial = partial[half:] + got
        bit *= 2
    return partial


def send_first_order(count, size):
    me = lax.axis_index("vocab")
    place = jnp.arange(count, dtype=jnp.int32)
    canon = jnp.zeros((count,), jnp.int32)
    first = jnp.int32(0)
    span, bit, level = count, 1, 0
    while bit < size:
        span //= 2
        side = (me // bit) % 2
        digit = (place // span) % 2
        canon = canon + ((1 - side) ^ digit) * span
        first = first + side * span
        bit *= 2
        level += 1
    return canon + place % span, first


def merge_pair(stats, other):
    top = jnp.maximum(stats[0], other[0])
    total = stats[1] * jnp.exp(stats[0] - top) + other[1] * jnp.exp(other[0] - top)
    return jnp.stack([top, total, stats[2] + other[2]])


def merge_stats(stats, size):
    bit = 1
    while bit < size:
        if bit * 4 <= size:
            got = [lax.ppermute(stats, "dp", [(i, i ^ (bit * k)) for i in range(size)]) for k in (1, 2, 3)]
            stats = merge_pair(merge_pair(stats, got[0]), merge_pair(got[1], got[2]))
            bit *= 4
        else:
            stats = merge_pair(stats, lax.ppermute(stats, "dp", [(i, i ^ bit) for i in range(size)]))
            bit *= 2
    return stats


def doubling_gather(values, first, size):
    me = lax.axis_index("vocab")
    total = values.shape[0] * size
    out = jnp.zeros((total,), values.dtype)
    out = lax.dynamic_update_slice(out, values, (first,))
    bit = 1
    while bit < size:
        other = lax.ppermute(out, "vocab", [(i, i ^ bit) for i in range(size)])
        out = out + other
        bit *= 2
    return out


def make_body(ring):
    def on_device(hidden, head_weight, lengths, targets, policy_logprobs):
        row_count = hidden.shape[0]
        dp_size = lax.axis_size("dp")
        vocab_size = lax.axis_size("vocab")
        all_rows = row_count * dp_size
        slot_count = all_rows // MB
        tile_width = head_weight.shape[1]
        col_start = lax.axis_index("dp") * tile_width
        live_count = all_rows * 5 // 8
        ends = jnp.cumsum(lengths)
        starts = ends - lengths
        packed, first = send_first_order(live_count, vocab_size)
        batch_hit = ends[:, None] <= packed[None, :]
        batch_of = jnp.sum(batch_hit.astype(jnp.int32), axis=0)
        in_batch = packed - jnp.sum(jnp.where(batch_of[None, :] == jnp.arange(MB, dtype=jnp.int32)[:, None], starts[:, None], 0), axis=0)
        live_rows = batch_of * slot_count + in_batch
        full_rows = ring_gather(hidden, ring, live_rows)
        share = live_count // vocab_size
        row_targets = lax.dynamic_slice_in_dim(live_rows, live_count - share, share)
        row_targets = jnp.take(targets, row_targets)
        pieces = 2 if tile_width % 256 == 0 else 1
        width = tile_width // pieces
        halves = lax.optimization_barrier(tuple(head_weight[:, piece * width:(piece + 1) * width] for piece in range(pieces)))
        parts = []
        for piece in range(pieces):
            partial = jnp.dot(full_rows, halves[piece], preferred_element_type=jnp.float32)
            logits = halving_scatter(partial, vocab_size)
            highest = jnp.max(logits, axis=1)
            exp_total = jnp.sum(jnp.exp(logits - highest[:, None]), axis=1)
            columns = col_start + piece * width + lax.broadcasted_iota(jnp.int32, logits.shape, 1)
            picked = jnp.sum(jnp.where(columns == row_targets[:, None], logits, 0.0), axis=1)
            parts.append((highest, exp_total, picked))
        highest = parts[0][0]
        for part in parts[1:]:
            highest = jnp.maximum(highest, part[0])
        exp_total = sum(part[1] * jnp.exp(part[0] - highest) for part in parts)
        picked = sum(part[2] for part in parts)
        stats = merge_stats(jnp.stack([highest, exp_total, picked]), dp_size)
        logprob = stats[2] - (stats[0] + jnp.log(stats[1]))
        all_values = doubling_gather(logprob, first, vocab_size)
        own_rows = lax.axis_index("dp") * row_count + jnp.arange(row_count, dtype=jnp.int32)
        own_batch = own_rows // slot_count
        is_live = own_rows % slot_count < jnp.take(lengths, own_batch)
        own_slot = jnp.clip(jnp.take(starts, own_batch) + own_rows % slot_count, 0, live_count - 1)
        own_values = jnp.take(all_values, own_slot)
        ref_logprob = jnp.where(is_live, own_values, 0.0)
        ratio_log = jnp.clip(ref_logprob - policy_logprobs, -20.0, 20.0)
        kl_value = jnp.where(is_live, jnp.minimum(jnp.exp(ratio_log) - ratio_log - 1.0, 10.0), 0.0)
        return (ref_logprob, kl_value)

    return on_device


def solution(mesh):
    return jax.shard_map(
        make_body(dp_ring(mesh)),
        mesh=mesh,
        in_specs=(P("dp", "vocab"), P("vocab", "dp"), P(), P(), P("dp")),
        out_specs=(P("dp"), P("dp")),
        check_vma=False,
    )
```

```python
import numpy as np
import jax
import jax.numpy as jnp
from jax import lax
from jax.sharding import PartitionSpec as P

MB = 8


def dp_ring(mesh):
    size = mesh.shape["dp"]
    try:
        coords = [tuple(dev.coords) for dev in mesh.devices[:, 0]]
        xs = sorted({c[0] for c in coords})
        zs = sorted({c[2] for c in coords})
        if len(xs) * len(zs) != size or len(zs) % 2:
            raise ValueError
        where = {(c[0], c[2]): i for i, c in enumerate(coords)}
        order = [where[(xs[0], z)] for z in zs]
        for row, z in enumerate(reversed(zs)):
            cols = xs[1:] if row % 2 == 0 else list(reversed(xs[1:]))
            order += [where[(x, z)] for x in cols]
        if sorted(order) != list(range(size)):
            raise ValueError
        return order
    except Exception:
        return list(range(size))


def ring_gather(block, ring, rows):
    size = len(ring)
    pos_of = np.argsort(np.asarray(ring))
    fwd = [(ring[i], ring[(i + 1) % size]) for i in range(size)]
    bwd = [(ring[(i + 1) % size], ring[i]) for i in range(size)]
    slots = [None] * size
    slots[0] = block
    ahead, behind = block, block
    for step in range(1, size // 2 + 1):
        ahead = lax.ppermute(ahead, "dp", fwd)
        slots[step] = ahead
        if step < size - step:
            behind = lax.ppermute(behind, "dp", bwd)
            slots[size - step] = behind
    count = block.shape[0]
    stacked = jnp.stack(slots).reshape(-1, block.shape[1])
    me = jnp.asarray(pos_of, jnp.int32)[lax.axis_index("dp")]
    slot_of = (me - jnp.asarray(pos_of, jnp.int32)) % size
    owner = rows // count
    hit = owner[None, :] == jnp.arange(size, dtype=jnp.int32)[:, None]
    where = jnp.sum(jnp.where(hit, slot_of[:, None], 0), axis=0) * count + rows % count
    choose = lax.broadcasted_iota(jnp.int32, (stacked.shape[0], where.shape[0]), 0) == where[None, :]
    picked = lax.dot_general(choose.astype(stacked.dtype), stacked, (((0,), (0,)), ((), ())), preferred_element_type=jnp.float32)
    return lax.optimization_barrier(picked.astype(stacked.dtype))


def halving_scatter(partial, size):
    me = lax.axis_index("vocab")
    first = jnp.int32(0)
    bit = 1
    while bit < size:
        half = partial.shape[0] // 2
        pairs = partial.reshape(2, half, partial.shape[1])
        side = (me // bit) % 2
        keep = jnp.take(pairs, side, axis=0)
        send = jnp.take(pairs, 1 - side, axis=0)
        got = lax.ppermute(send, "vocab", [(i, i ^ bit) for i in range(size)])
        partial = keep + got
        first = first + side * half
        bit *= 2
    return partial, first


def merge_pair(stats, other):
    top = jnp.maximum(stats[0], other[0])
    total = stats[1] * jnp.exp(stats[0] - top) + other[1] * jnp.exp(other[0] - top)
    return jnp.stack([top, total, stats[2] + other[2]])


def merge_stats(stats, size):
    bit = 1
    while bit < size:
        if bit * 4 <= size:
            got = [lax.ppermute(stats, "dp", [(i, i ^ (bit * k)) for i in range(size)]) for k in (1, 2, 3)]
            stats = merge_pair(merge_pair(stats, got[0]), merge_pair(got[1], got[2]))
            bit *= 4
        else:
            stats = merge_pair(stats, lax.ppermute(stats, "dp", [(i, i ^ bit) for i in range(size)]))
            bit *= 2
    return stats


def doubling_gather(values, first, size):
    me = lax.axis_index("vocab")
    total = values.shape[0] * size
    out = jnp.zeros((total,), values.dtype)
    out = lax.dynamic_update_slice(out, values, (first,))
    bit = 1
    while bit < size:
        other = lax.ppermute(out, "vocab", [(i, i ^ bit) for i in range(size)])
        out = out + other
        bit *= 2
    return out


def make_body(ring):
    def on_device(hidden, head_weight, lengths, targets, policy_logprobs):
        row_count = hidden.shape[0]
        dp_size = lax.axis_size("dp")
        vocab_size = lax.axis_size("vocab")
        all_rows = row_count * dp_size
        slot_count = all_rows // MB
        tile_width = head_weight.shape[1]
        col_start = lax.axis_index("dp") * tile_width
        live_count = all_rows * 5 // 8
        ends = jnp.cumsum(lengths)
        starts = ends - lengths
        packed = jnp.arange(live_count, dtype=jnp.int32)
        batch_hit = ends[:, None] <= packed[None, :]
        batch_of = jnp.sum(batch_hit.astype(jnp.int32), axis=0)
        in_batch = packed - jnp.sum(jnp.where(batch_of[None, :] == jnp.arange(MB, dtype=jnp.int32)[:, None], starts[:, None], 0), axis=0)
        live_rows = batch_of * slot_count + in_batch
        full_rows = ring_gather(hidden, ring, live_rows)
        partial = jnp.dot(full_rows, head_weight, preferred_element_type=jnp.float32)
        logits, first = halving_scatter(partial, vocab_size)
        share = logits.shape[0]
        row_targets = jnp.take(targets, lax.dynamic_slice_in_dim(live_rows, first, share))
        highest = jnp.max(logits, axis=1)
        exp_total = jnp.sum(jnp.exp(logits - highest[:, None]), axis=1)
        columns = col_start + lax.broadcasted_iota(jnp.int32, logits.shape, 1)
        picked = jnp.sum(jnp.where(columns == row_targets[:, None], logits, 0.0), axis=1)
        stats = merge_stats(jnp.stack([highest, exp_total, picked]), dp_size)
        logprob = stats[2] - (stats[0] + jnp.log(stats[1]))
        all_values = doubling_gather(logprob, first, vocab_size)
        own_rows = lax.axis_index("dp") * row_count + jnp.arange(row_count, dtype=jnp.int32)
        own_batch = own_rows // slot_count
        is_live = own_rows % slot_count < jnp.take(lengths, own_batch)
        own_slot = jnp.clip(jnp.take(starts, own_batch) + own_rows % slot_count, 0, live_count - 1)
        own_values = jnp.sum(jnp.where(own_slot[:, None] == jnp.arange(live_count, dtype=jnp.int32)[None, :], all_values[None, :], 0.0), axis=1)
        ref_logprob = jnp.where(is_live, own_values, 0.0)
        ratio_log = jnp.clip(ref_logprob - policy_logprobs, -20.0, 20.0)
        kl_value = jnp.where(is_live, jnp.minimum(jnp.exp(ratio_log) - ratio_log - 1.0, 10.0), 0.0)
        return (ref_logprob, kl_value)

    return on_device


def solution(mesh):
    return jax.shard_map(
        make_body(dp_ring(mesh)),
        mesh=mesh,
        in_specs=(P("dp", "vocab"), P("vocab", "dp"), P(), P(), P("dp")),
        out_specs=(P("dp"), P("dp")),
        check_vma=False,
    )
```

```python
import numpy as np
import jax
import jax.numpy as jnp
from jax import lax
from jax.sharding import PartitionSpec as P

MB = 8


def dp_ring(mesh):
    size = mesh.shape["dp"]
    try:
        coords = [tuple(dev.coords) for dev in mesh.devices[:, 0]]
        xs = sorted({c[0] for c in coords})
        zs = sorted({c[2] for c in coords})
        if len(xs) * len(zs) != size or len(zs) % 2:
            raise ValueError
        where = {(c[0], c[2]): i for i, c in enumerate(coords)}
        order = [where[(xs[0], z)] for z in zs]
        for row, z in enumerate(reversed(zs)):
            cols = xs[1:] if row % 2 == 0 else list(reversed(xs[1:]))
            order += [where[(x, z)] for x in cols]
        if sorted(order) != list(range(size)):
            raise ValueError
        return order
    except Exception:
        return list(range(size))


def ring_gather(block, ring, rows):
    size = len(ring)
    pos_of = np.argsort(np.asarray(ring))
    fwd = [(ring[i], ring[(i + 1) % size]) for i in range(size)]
    bwd = [(ring[(i + 1) % size], ring[i]) for i in range(size)]
    slots = [None] * size
    slots[0] = block
    ahead, behind = block, block
    for step in range(1, size // 2 + 1):
        ahead = lax.ppermute(ahead, "dp", fwd)
        slots[step] = ahead
        if step < size - step:
            behind = lax.ppermute(behind, "dp", bwd)
            slots[size - step] = behind
    count = block.shape[0]
    stacked = jnp.stack(slots).reshape(-1, block.shape[1])
    me = jnp.asarray(pos_of, jnp.int32)[lax.axis_index("dp")]
    slot_of = (me - jnp.asarray(pos_of, jnp.int32)) % size
    owner = rows // count
    hit = owner[None, :] == jnp.arange(size, dtype=jnp.int32)[:, None]
    where = jnp.sum(jnp.where(hit, slot_of[:, None], 0), axis=0) * count + rows % count
    choose = lax.broadcasted_iota(jnp.int32, (stacked.shape[0], where.shape[0]), 0) == where[None, :]
    picked = lax.dot_general(choose.astype(stacked.dtype), stacked, (((0,), (0,)), ((), ())), preferred_element_type=jnp.float32)
    return lax.optimization_barrier(picked.astype(stacked.dtype))


def halving_scatter(partial, size):
    me = lax.axis_index("vocab")
    first = jnp.int32(0)
    bit = 1
    while bit < size:
        half = partial.shape[0] // 2
        pairs = partial.reshape(2, half, partial.shape[1])
        side = (me // bit) % 2
        keep = jnp.take(pairs, side, axis=0)
        send = jnp.take(pairs, 1 - side, axis=0)
        got = lax.ppermute(send, "vocab", [(i, i ^ bit) for i in range(size)])
        partial = keep + got
        first = first + side * half
        bit *= 2
    return partial, first


def merge_pair(stats, other):
    top = jnp.maximum(stats[0], other[0])
    total = stats[1] * jnp.exp(stats[0] - top) + other[1] * jnp.exp(other[0] - top)
    return jnp.stack([top, total, stats[2] + other[2]])


def merge_stats(stats, size):
    bit = 1
    while bit < size:
        if bit * 4 <= size:
            got = [lax.ppermute(stats, "dp", [(i, i ^ (bit * k)) for i in range(size)]) for k in (1, 2, 3)]
            stats = merge_pair(merge_pair(stats, got[0]), merge_pair(got[1], got[2]))
            bit *= 4
        else:
            stats = merge_pair(stats, lax.ppermute(stats, "dp", [(i, i ^ bit) for i in range(size)]))
            bit *= 2
    return stats


def doubling_gather(values, first, size):
    total = values.shape[0] * size
    out = jnp.zeros((total,), values.dtype)
    out = lax.dynamic_update_slice(out, values, (first,))
    bit = 1
    other = jnp.zeros_like(out)
    while bit < size:
        if bit * 2 >= size:
            other = lax.ppermute(out, "vocab", [(i, i ^ bit) for i in range(size)])
        else:
            out = out + lax.ppermute(out, "vocab", [(i, i ^ bit) for i in range(size)])
        bit *= 2
    return out, other


def make_body(ring):
    def on_device(hidden, head_weight, lengths, targets, policy_logprobs):
        row_count = hidden.shape[0]
        dp_size = lax.axis_size("dp")
        vocab_size = lax.axis_size("vocab")
        all_rows = row_count * dp_size
        slot_count = all_rows // MB
        tile_width = head_weight.shape[1]
        col_start = lax.axis_index("dp") * tile_width
        live_count = all_rows * 5 // 8
        ends = jnp.cumsum(lengths)
        starts = ends - lengths
        packed = jnp.arange(live_count, dtype=jnp.int32)
        batch_hit = ends[:, None] <= packed[None, :]
        batch_of = jnp.sum(batch_hit.astype(jnp.int32), axis=0)
        in_batch = packed - jnp.sum(jnp.where(batch_of[None, :] == jnp.arange(MB, dtype=jnp.int32)[:, None], starts[:, None], 0), axis=0)
        live_rows = batch_of * slot_count + in_batch
        full_rows = ring_gather(hidden, ring, live_rows)
        partial = jnp.dot(full_rows, head_weight, preferred_element_type=jnp.float32)
        logits, first = halving_scatter(partial, vocab_size)
        share = logits.shape[0]
        row_targets = jnp.take(targets, lax.dynamic_slice_in_dim(live_rows, first, share))
        highest = jnp.max(logits, axis=1)
        exp_total = jnp.sum(jnp.exp(logits - highest[:, None]), axis=1)
        columns = col_start + lax.broadcasted_iota(jnp.int32, logits.shape, 1)
        picked = jnp.sum(jnp.where(columns == row_targets[:, None], logits, 0.0), axis=1)
        stats = merge_stats(jnp.stack([highest, exp_total, picked]), dp_size)
        logprob = stats[2] - (stats[0] + jnp.log(stats[1]))
        mine, theirs = doubling_gather(logprob, first, vocab_size)
        own_rows = lax.axis_index("dp") * row_count + jnp.arange(row_count, dtype=jnp.int32)
        own_batch = own_rows // slot_count
        is_live = own_rows % slot_count < jnp.take(lengths, own_batch)
        own_slot = jnp.clip(jnp.take(starts, own_batch) + own_rows % slot_count, 0, live_count - 1)
        own_hit = own_slot[:, None] == jnp.arange(live_count, dtype=jnp.int32)[None, :]
        own_values = jnp.sum(jnp.where(own_hit, mine[None, :], 0.0), axis=1) + jnp.sum(jnp.where(own_hit, theirs[None, :], 0.0), axis=1)
        ref_logprob = jnp.where(is_live, own_values, 0.0)
        ratio_log = jnp.clip(ref_logprob - policy_logprobs, -20.0, 20.0)
        kl_value = jnp.where(is_live, jnp.minimum(jnp.exp(ratio_log) - ratio_log - 1.0, 10.0), 0.0)
        return (ref_logprob, kl_value)

    return on_device


def solution(mesh):
    return jax.shard_map(
        make_body(dp_ring(mesh)),
        mesh=mesh,
        in_specs=(P("dp", "vocab"), P("vocab", "dp"), P(), P(), P("dp")),
        out_specs=(P("dp"), P("dp")),
        check_vma=False,
    )
```
